768 devices in a mesh: seq: 16 (over x, y_lo), grp: 48 (over z, y_hi, core).
Axes of the slice: x: 4, y: 8 (y_hi: 2, y_lo: 4; y = y_hi * 4 + y_lo), z: 12, core: 2. Of those that a mesh axis runs over, the one named last changes fastest.
Arguments:
- embeddings: bfloat16 [16, 48, 512, 1024], P('seq', 'grp'), may hold values from -8 to 8
- seed_labels: float32 [16, 48, 512, 128], P('seq', 'grp'), may hold values from -8 to 8
- sources: int32 [16, 48, 3, 4], P('seq', 'grp'), may hold values from -1 to 47, as said below
- counts: int32 [16, 48], P('seq', 'grp'), may hold values from 4 to 8
Outputs:
- diffused: float32 [16, 48, 512, 128], P('seq', 'grp')
The draws below stay inside these ranges and needn't reach their ends.
Inputs may be any that keep to these rules, and one draw needn't show every extreme that they name: `sources`: an entry at [q,g,s,j] is -1 or the group of a source block at the same seq index q in another group than g; the entries other than -1 in one list are distinct, come before the -1 entries, and some list is full in every draw.
All inputs are finite; a program needn't handle non-finite values.
Results may differ from the reference program's by a relative error of at most 0.0006.
Values may be sent and summed in bfloat16 or wider, within the bound.
No kernel may reach another device: no remote copies, remote signals or barrier semaphores. Data moves between devices by JAX's collectives and lax.ppermute only.
A program may use at most 32 MiB of HBM per device.

```python
import jax
import jax.numpy as jnp
from jax import lax

D = 1024
C = 128
ROWS = 512
CLUS = 32
STEPS = 3
SLOTS = 4
N_SEQ = 16
N_GRP = 48


def cluster_rows(key):
    cluster_ids = jax.random.randint(jax.random.fold_in(key, 11), (N_SEQ, N_GRP, ROWS // CLUS), 0, 64)
    return jnp.broadcast_to(cluster_ids[..., None], (N_SEQ, N_GRP, ROWS // CLUS, CLUS)).reshape(N_SEQ, N_GRP, ROWS)


def draw_embeddings(key, part):
    row_ids = cluster_rows(key)
    prototypes = jnp.clip(jax.random.normal(jax.random.fold_in(key, 12), (64, D), jnp.float32), -4.0, 4.0)
    base = prototypes[row_ids]
    noise = jnp.clip(jax.random.normal(jax.random.fold_in(key, 16), (N_SEQ, N_GRP, ROWS, D), jnp.float32), -4.0, 4.0)
    values = base + 0.6 * noise
    return jnp.clip(values, -8.0, 8.0).astype(jnp.bfloat16)


def draw_seed_labels(key, part):
    row_ids = cluster_rows(key)
    prototypes = jnp.clip(jax.random.normal(jax.random.fold_in(key, 17), (64, C), jnp.float32), -3.0, 3.0)
    base = prototypes[row_ids]
    noise = jnp.clip(jax.random.normal(jax.random.fold_in(key, 19), (N_SEQ, N_GRP, ROWS, C), jnp.float32), -3.0, 3.0)
    values = base + 0.7 * noise
    return jnp.clip(values, -8.0, 8.0).astype(jnp.float32)


def draw_sources(key, part):
    others = N_GRP - 1
    scores = jax.random.randint(jax.random.fold_in(key, 21), (N_SEQ, N_GRP, STEPS, others), 0, 1048576) * others
    scores = scores + jnp.arange(others, dtype=jnp.int32)
    order = jnp.argsort(scores, axis=-1, stable=True)[..., :SLOTS].astype(jnp.int32)
    owner = jnp.arange(N_GRP, dtype=jnp.int32)[None, :, None, None]
    picked = (owner + 1 + order) % N_GRP
    live = jax.random.randint(jax.random.fold_in(key, 22), (N_SEQ, N_GRP, STEPS, 1), 0, SLOTS + 1)
    total = N_SEQ * N_GRP * STEPS
    chosen_list = jax.random.randint(jax.random.fold_in(key, 23), (), 0, total)
    flat_index = jnp.arange(total, dtype=jnp.int32).reshape(N_SEQ, N_GRP, STEPS, 1)
    live = jnp.where(flat_index == chosen_list, SLOTS, live)
    slot_index = jnp.arange(SLOTS, dtype=jnp.int32)
    return jnp.where(slot_index < live, picked, -1).astype(jnp.int32)


def with_ends(array, stream_key, smallest, largest):
    place = [jax.random.randint(jax.random.fold_in(stream_key, axis), (), 0, length) for axis, length in enumerate(array.shape)]
    longest = array.shape.index(max(array.shape))
    beside = place[:longest] + [(place[longest] + 1) % array.shape[longest]] + place[longest + 1:]
    return array.at[tuple(place)].set(smallest).at[tuple(beside)].set(largest)


def setup_inputs(seed: int = 0) -> dict:
    splits = jax.random.split(jax.random.key(seed), 5)
    return {
        "embeddings": draw_embeddings(jax.random.fold_in(splits[4], 71), 0),
        "seed_labels": draw_seed_labels(jax.random.fold_in(splits[4], 71), 0),
        "sources": draw_sources(jax.random.fold_in(splits[4], 71), 0),
        "counts": with_ends(jax.random.randint(splits[3], (N_SEQ, N_GRP), SLOTS, 2 * SLOTS + 1), jax.random.fold_in(splits[3], 1), SLOTS, 2 * SLOTS).astype(jnp.int32),
    }


tile_scale = 8.0
pair_scale = 2.0
keep_share = 0.2
eps = 1e-06
highest = lax.Precision.HIGHEST

def normalized(values):
    floats = values.astype(jnp.float32)
    return (floats * lax.rsqrt(lax.optimization_barrier(jnp.sum(floats * floats, axis=-1, keepdims=True)) + eps)).astype(jnp.bfloat16)

def kernel_tile(left, right, blank):
    score = jnp.dot(left, right.T, preferred_element_type=jnp.float32)
    weights = jnp.exp(tile_scale * (score - 1.0))
    if blank:
        weights = weights * (1.0 - jnp.eye(left.shape[0], dtype=jnp.float32))
    return weights.astype(jnp.bfloat16)

def build_self(block):
    tile = kernel_tile(block, block, True)
    return (tile, lax.optimization_barrier(jnp.sum(tile, axis=1, dtype=jnp.float32)))

def build_next(pair):
    tile = kernel_tile(pair[0], pair[1], False)
    return (tile, lax.optimization_barrier(jnp.sum(tile, axis=1, dtype=jnp.float32)), lax.optimization_barrier(jnp.sum(tile, axis=0, dtype=jnp.float32)))

def local_terms(pack):
    self_tile, next_tile, mine, ahead = pack
    return jnp.dot(self_tile, mine, preferred_element_type=jnp.float32) + jnp.dot(next_tile, ahead, preferred_element_type=jnp.float32)

def back_terms(pack):
    next_tile, mine = pack
    return lax.dot_general(next_tile, mine, (((0,), (0,)), ((), ())), preferred_element_type=jnp.float32)

def reference(embeddings, seed_labels, sources, counts):
    blocks = N_SEQ * N_GRP
    unit_emb = normalized(embeddings)
    flat_unit = unit_emb.reshape(blocks, ROWS, D)
    after_unit = jnp.roll(unit_emb, -1, axis=0).reshape(blocks, ROWS, D)
    self_tiles, self_rows = lax.map(build_self, flat_unit)
    next_tiles, next_rows, next_cols = lax.map(build_next, (flat_unit, after_unit))
    prior_cols = jnp.roll(next_cols.reshape(N_SEQ, N_GRP, ROWS), 1, axis=0)
    degree = self_rows.reshape(N_SEQ, N_GRP, ROWS) + next_rows.reshape(N_SEQ, N_GRP, ROWS) + prior_cols
    centre = lax.optimization_barrier(jnp.mean(unit_emb, axis=2, dtype=jnp.float32))
    centre_unit = centre * lax.rsqrt(lax.optimization_barrier(jnp.sum(centre * centre, axis=-1, keepdims=True)) + eps)
    similar = jnp.einsum('qgd,qhd->qgh', centre_unit, centre_unit, precision=highest)
    pair_weight = jnp.exp(pair_scale * similar)
    member = jnp.arange(N_GRP, dtype=jnp.int32)
    count_value = counts.astype(jnp.float32)
    labels = seed_labels
    for iteration in range(STEPS):
        label_bf = labels.astype(jnp.bfloat16)
        flat_labels = label_bf.reshape(blocks, ROWS, C)
        ahead_labels = jnp.roll(label_bf, -1, axis=0).reshape(blocks, ROWS, C)
        local = lax.map(local_terms, (self_tiles, next_tiles, flat_labels, ahead_labels)).reshape(N_SEQ, N_GRP, ROWS, C)
        backward = lax.map(back_terms, (next_tiles, flat_labels)).reshape(N_SEQ, N_GRP, ROWS, C)
        backward = jnp.roll(backward, 1, axis=0)
        spread = (local + backward) / degree[..., None]
        summary = lax.optimization_barrier(jnp.sum(labels.reshape(N_SEQ, N_GRP, ROWS // CLUS, CLUS, C), axis=3)) / CLUS
        chosen = lax.optimization_barrier(jnp.sum((sources[:, :, iteration, :, None] == member).astype(jnp.float32), axis=2))
        coefficient = chosen * pair_weight / count_value[..., None]
        far = jnp.einsum('qgh,qhkc->qgkc', coefficient, summary, precision=highest)
        far_rows = jnp.broadcast_to(far[:, :, :, None, :], (N_SEQ, N_GRP, ROWS // CLUS, CLUS, C)).reshape(N_SEQ, N_GRP, ROWS, C)
        labels = keep_share * seed_labels + (1.0 - keep_share) * (spread + far_rows)
    return labels
```

```python
import numpy as np
import jax
import jax.numpy as jnp
from jax import lax
from jax.sharding import Mesh, PartitionSpec as P

CLUS = 32
STEPS = 3


tile_scale = 8.0
pair_scale = 2.0
keep_share = 0.2
eps = 1e-06
highest = lax.Precision.HIGHEST

GRP_PARTS = ("grp_z", "grp_y", "grp_c")


def padded(block, sides, width):
    for axis, dim in sides:
        count = lax.axis_size(axis)
        forward = [(i, i + 1) for i in range(count - 1)]
        forward.append((count - 1, 0))
        backward = [(target, source) for source, target in forward]
        low = lax.ppermute(
            lax.slice_in_dim(block, block.shape[dim] - width, None, axis=dim), axis, forward
        )
        high = lax.ppermute(lax.slice_in_dim(block, 0, width, axis=dim), axis, backward)
        block = jnp.concatenate([low, block, high], axis=dim)
    return block


def gather_groups(value):
    for axis in reversed(GRP_PARTS):
        value = lax.all_gather(value, axis, axis=0, tiled=True)
    return value


def normalized(values):
    floats = values.astype(jnp.float32)
    return (floats * lax.rsqrt(jnp.sum(floats * floats, axis=-1, keepdims=True) + eps)).astype(
        jnp.bfloat16
    )


def kernel_tile(left, right, blank):
    score = jnp.dot(left, right.T, preferred_element_type=jnp.float32)
    weights = jnp.exp(tile_scale * (score - 1.0))
    if blank:
        weights = weights * (1.0 - jnp.eye(left.shape[0], dtype=jnp.float32))
    return weights.astype(jnp.bfloat16)


def body(groups, embeddings, seed_labels, sources, counts):
    row_count = embeddings.shape[2]
    classes = seed_labels.shape[3]
    width = embeddings.shape[3]
    unit_emb = normalized(embeddings[0, 0])
    self_tile = kernel_tile(unit_emb, unit_emb, True)
    self_rows = jnp.sum(self_tile, axis=1, dtype=jnp.float32)
    centre = jnp.mean(unit_emb, axis=0, dtype=jnp.float32)
    centre_unit = centre * lax.rsqrt(jnp.sum(centre * centre) + eps)
    seed = seed_labels[0, 0]
    coarse_count = row_count // CLUS
    centre_rows = width // classes

    def summarize(labels):
        return jnp.sum(labels.reshape(coarse_count, CLUS, classes), axis=1) / CLUS

    first = gather_groups(
        jnp.concatenate([centre_unit.reshape(centre_rows, classes), summarize(seed)])[None]
    )
    table = first[:, :centre_rows].reshape(groups, width)
    pair_weight = jnp.exp(pair_scale * jnp.dot(table, centre_unit, precision=highest))
    extended = padded(unit_emb, (("seq", 0),), row_count)
    before_unit = extended[:row_count]
    after_unit = extended[2 * row_count :]
    next_tile = kernel_tile(unit_emb, after_unit, False)
    prior_tile = kernel_tile(unit_emb, before_unit, False)
    degree = (
        self_rows
        + jnp.sum(next_tile, axis=1, dtype=jnp.float32)
        + jnp.sum(prior_tile, axis=1, dtype=jnp.float32)
    )
    labels = seed
    count_value = counts[0, 0].astype(jnp.float32)
    member = jnp.arange(groups, dtype=jnp.int32)
    for iteration in range(STEPS):
        label_bf = labels.astype(jnp.bfloat16)
        widened = padded(label_bf, (("seq", 0),), row_count)
        local = jnp.dot(self_tile, label_bf, preferred_element_type=jnp.float32) + jnp.dot(
            next_tile, widened[2 * row_count :], preferred_element_type=jnp.float32
        )
        local = local + jnp.dot(prior_tile, widened[:row_count], preferred_element_type=jnp.float32)
        spread = local / degree[:, None]
        if iteration == 0:
            gathered = first[:, centre_rows:]
        else:
            gathered = gather_groups(summarize(labels)[None])
        chosen = jnp.sum(
            (sources[0, 0, iteration][:, None] == member[None, :]).astype(jnp.float32), axis=0
        )
        coefficient = chosen * pair_weight / count_value
        far = jnp.einsum("h,hkc->kc", coefficient, gathered, precision=highest)
        far_rows = jnp.broadcast_to(far[:, None, :], (coarse_count, CLUS, classes)).reshape(
            row_count, classes
        )
        labels = keep_share * seed + (1.0 - keep_share) * (spread + far_rows)
    return labels[None, None]


def solution(mesh):
    groups = mesh.shape["grp"]
    devices = np.asarray(mesh.devices)
    if groups % 4 == 0:
        parts = (groups // 4, 2, 2)
    else:
        parts = (groups, 1, 1)
    split = Mesh(devices.reshape((mesh.shape["seq"],) + parts), ("seq",) + GRP_PARTS)
    block = P("seq", GRP_PARTS, None, None)
    return jax.shard_map(
        lambda *args: body(groups, *args),
        mesh=split,
        in_specs=(block, block, block, P("seq", GRP_PARTS)),
        out_specs=block,
        check_vma=False,
    )
```

```python
import numpy as np
import jax
import jax.numpy as jnp
from jax import lax
from jax.sharding import Mesh, PartitionSpec as P

CLUS = 32
STEPS = 3


tile_scale = 8.0
pair_scale = 2.0
keep_share = 0.2
eps = 1e-06
highest = lax.Precision.HIGHEST

GRP_PARTS = ("grp_z", "grp_y", "grp_c")


def padded(block, sides, width):
    for axis, dim in sides:
        count = lax.axis_size(axis)
        forward = [(i, i + 1) for i in range(count - 1)]
        forward.append((count - 1, 0))
        backward = [(target, source) for source, target in forward]
        low = lax.ppermute(
            lax.slice_in_dim(block, block.shape[dim] - width, None, axis=dim), axis, forward
        )
        high = lax.ppermute(lax.slice_in_dim(block, 0, width, axis=dim), axis, backward)
        block = jnp.concatenate([low, block, high], axis=dim)
    return block


def gather_groups(value):
    for axis in reversed(GRP_PARTS):
        value = lax.all_gather(value, axis, axis=0, tiled=True)
    return value


def normalized(values):
    floats = values.astype(jnp.float32)
    return (floats * lax.rsqrt(jnp.sum(floats * floats, axis=-1, keepdims=True) + eps)).astype(
        jnp.bfloat16
    )


def kernel_tile(left, right, blank):
    score = jnp.dot(left, right.T, preferred_element_type=jnp.float32)
    weights = jnp.exp(tile_scale * (score - 1.0))
    if blank:
        weights = weights * (1.0 - jnp.eye(left.shape[0], dtype=jnp.float32))
    return weights.astype(jnp.bfloat16)


def body(groups, embeddings, seed_labels, sources, counts):
    row_count = embeddings.shape[2]
    classes = seed_labels.shape[3]
    width = embeddings.shape[3]
    unit_emb = normalized(embeddings[0, 0])
    self_tile = kernel_tile(unit_emb, unit_emb, True)
    self_rows = jnp.sum(self_tile, axis=1, dtype=jnp.float32)
    centre = jnp.mean(unit_emb, axis=0, dtype=jnp.float32)
    centre_unit = centre * lax.rsqrt(jnp.sum(centre * centre) + eps)
    seed = seed_labels[0, 0]
    coarse_count = row_count // CLUS
    centre_rows = width // classes

    def summarize(labels):
        return jnp.sum(labels.reshape(coarse_count, CLUS, classes), axis=1) / CLUS

    first = gather_groups(
        jnp.concatenate([centre_unit.reshape(centre_rows, classes), summarize(seed)])[None]
    )
    table = first[:, :centre_rows].reshape(groups, width)
    pair_weight = jnp.exp(pair_scale * jnp.dot(table, centre_unit, precision=highest))
    unit_send, first = lax.optimization_barrier((unit_emb, first))
    extended = padded(unit_send, (("seq", 0),), row_count)
    before_unit = extended[:row_count]
    after_unit = extended[2 * row_count :]
    next_tile = kernel_tile(unit_emb, after_unit, False)
    prior_tile = kernel_tile(unit_emb, before_unit, False)
    degree = (
        self_rows
        + jnp.sum(next_tile, axis=1, dtype=jnp.float32)
        + jnp.sum(prior_tile, axis=1, dtype=jnp.float32)
    )
    labels = seed
    count_value = counts[0, 0].astype(jnp.float32)
    member = jnp.arange(groups, dtype=jnp.int32)
    for iteration in range(STEPS):
        label_bf = labels.astype(jnp.bfloat16)
        widened = padded(label_bf, (("seq", 0),), row_count)
        local = jnp.dot(self_tile, label_bf, preferred_element_type=jnp.float32) + jnp.dot(
            next_tile, widened[2 * row_count :], preferred_element_type=jnp.float32
        )
        local = local + jnp.dot(prior_tile, widened[:row_count], preferred_element_type=jnp.float32)
        spread = local / degree[:, None]
        if iteration == 0:
            gathered = first[:, centre_rows:]
        else:
            gathered = gather_groups(summarize(labels)[None])
        chosen = jnp.sum(
            (sources[0, 0, iteration][:, None] == member[None, :]).astype(jnp.float32), axis=0
        )
        coefficient = chosen * pair_weight / count_value
        far = jnp.einsum("h,hkc->kc", coefficient, gathered, precision=highest)
        far_rows = jnp.broadcast_to(far[:, None, :], (coarse_count, CLUS, classes)).reshape(
            row_count, classes
        )
        labels = keep_share * seed + (1.0 - keep_share) * (spread + far_rows)
    return labels[None, None]


def solution(mesh):
    groups = mesh.shape["grp"]
    devices = np.asarray(mesh.devices)
    if groups % 4 == 0:
        parts = (groups // 4, 2, 2)
    else:
        parts = (groups, 1, 1)
    split = Mesh(devices.reshape((mesh.shape["seq"],) + parts), ("seq",) + GRP_PARTS)
    block = P("seq", GRP_PARTS, None, None)
    return jax.shard_map(
        lambda *args: body(groups, *args),
        mesh=split,
        in_specs=(block, block, block, P("seq", GRP_PARTS)),
        out_specs=block,
        check_vma=False,
    )
```

```python
import numpy as np
import jax
import jax.numpy as jnp
from jax import lax
from jax.sharding import Mesh, PartitionSpec as P

CLUS = 32
STEPS = 3


tile_scale = 8.0
pair_scale = 2.0
keep_share = 0.2
eps = 1e-06
highest = lax.Precision.HIGHEST

GRP_PARTS = ("grp_z", "grp_y", "grp_c")


def from_next(block):
    count = lax.axis_size("seq")
    return lax.ppermute(block, "seq", [((i + 1) % count, i) for i in range(count)])


def from_prev(block):
    count = lax.axis_size("seq")
    return lax.ppermute(block, "seq", [(i, (i + 1) % count) for i in range(count)])


def gather_groups(value):
    for axis in reversed(GRP_PARTS):
        value = lax.all_gather(value, axis, axis=0, tiled=True)
    return value


def normalized(values):
    floats = values.astype(jnp.float32)
    return (floats * lax.rsqrt(jnp.sum(floats * floats, axis=-1, keepdims=True) + eps)).astype(
        jnp.bfloat16
    )


def kernel_tile(left, right, blank):
    score = jnp.dot(left, right.T, preferred_element_type=jnp.float32)
    weights = jnp.exp(tile_scale * (score - 1.0))
    if blank:
        weights = weights * (1.0 - jnp.eye(left.shape[0], dtype=jnp.float32))
    return weights.astype(jnp.bfloat16)


def body(groups, embeddings, seed_labels, sources, counts):
    row_count = embeddings.shape[2]
    classes = seed_labels.shape[3]
    width = embeddings.shape[3]
    unit_emb = normalized(embeddings[0, 0])
    self_tile = kernel_tile(unit_emb, unit_emb, True)
    self_rows = jnp.sum(self_tile, axis=1, dtype=jnp.float32)
    centre = jnp.mean(unit_emb, axis=0, dtype=jnp.float32)
    centre_unit = centre * lax.rsqrt(jnp.sum(centre * centre) + eps)
    seed = seed_labels[0, 0]
    coarse_count = row_count // CLUS
    centre_rows = width // classes

    def summarize(labels):
        return jnp.sum(labels.reshape(coarse_count, CLUS, classes), axis=1) / CLUS

    first = gather_groups(
        jnp.concatenate([centre_unit.reshape(centre_rows, classes), summarize(seed)])[None]
    )
    table = first[:, :centre_rows].reshape(groups, width)
    pair_weight = jnp.exp(pair_scale * jnp.dot(table, centre_unit, precision=highest))
    unit_send, first = lax.optimization_barrier((unit_emb, first))
    after_unit = from_next(unit_send)
    next_tile = kernel_tile(unit_emb, after_unit, False)
    next_rows = jnp.sum(next_tile, axis=1, dtype=jnp.float32)
    next_cols = jnp.sum(next_tile, axis=0, dtype=jnp.float32)
    labels = seed
    count_value = counts[0, 0].astype(jnp.float32)
    member = jnp.arange(groups, dtype=jnp.int32)
    col_rows = row_count // classes
    for iteration in range(STEPS):
        label_bf = labels.astype(jnp.bfloat16)
        ahead = from_next(label_bf)
        back = lax.dot_general(
            next_tile, label_bf, (((0,), (0,)), ((), ())), preferred_element_type=jnp.float32
        )
        if iteration == 0:
            packet = from_prev(jnp.concatenate([back, next_cols.reshape(col_rows, classes)]))
            back_in = packet[:row_count]
            degree = self_rows + next_rows + packet[row_count:].reshape(row_count)
        else:
            back_in = from_prev(back)
        local = jnp.dot(self_tile, label_bf, preferred_element_type=jnp.float32) + jnp.dot(
            next_tile, ahead, preferred_element_type=jnp.float32
        )
        local = local + back_in
        spread = local / degree[:, None]
        if iteration == 0:
            gathered = first[:, centre_rows:]
        else:
            gathered = gather_groups(summarize(labels)[None])
        chosen = jnp.sum(
            (sources[0, 0, iteration][:, None] == member[None, :]).astype(jnp.float32), axis=0
        )
        coefficient = chosen * pair_weight / count_value
        far = jnp.einsum("h,hkc->kc", coefficient, gathered, precision=highest)
        far_rows = jnp.broadcast_to(far[:, None, :], (coarse_count, CLUS, classes)).reshape(
            row_count, classes
        )
        labels = keep_share * seed + (1.0 - keep_share) * (spread + far_rows)
    return labels[None, None]


def solution(mesh):
    groups = mesh.shape["grp"]
    devices = np.asarray(mesh.devices)
    if groups % 4 == 0:
        parts = (groups // 4, 2, 2)
    else:
        parts = (groups, 1, 1)
    split = Mesh(devices.reshape((mesh.shape["seq"],) + parts), ("seq",) + GRP_PARTS)
    block = P("seq", GRP_PARTS, None, None)
    return jax.shard_map(
        lambda *args: body(groups, *args),
        mesh=split,
        in_specs=(block, block, block, P("seq", GRP_PARTS)),
        out_specs=block,
        check_vma=False,
    )
```

```python
import numpy as np
import jax
import jax.numpy as jnp
from jax import lax
from jax.sharding import Mesh, PartitionSpec as P

CLUS = 32
STEPS = 3


tile_scale = 8.0
pair_scale = 2.0
keep_share = 0.2
eps = 1e-06
highest = lax.Precision.HIGHEST

GRP_PARTS = ("grp_z", "grp_y", "grp_c")


def from_next(block):
    count = lax.axis_size("seq")
    return lax.ppermute(block, "seq", [((i + 1) % count, i) for i in range(count)])


def from_prev(block):
    count = lax.axis_size("seq")
    return lax.ppermute(block, "seq", [(i, (i + 1) % count) for i in range(count)])


def gather_groups(value):
    for axis in reversed(GRP_PARTS):
        value = lax.all_gather(value, axis, axis=0, tiled=True)
    return value


def normalized(values):
    floats = values.astype(jnp.float32)
    return (floats * lax.rsqrt(jnp.sum(floats * floats, axis=-1, keepdims=True) + eps)).astype(
        jnp.bfloat16
    )


def kernel_tile(left, right, blank):
    score = jnp.dot(left, right.T, preferred_element_type=jnp.float32)
    weights = jnp.exp(tile_scale * (score - 1.0))
    if blank:
        weights = weights * (1.0 - jnp.eye(left.shape[0], dtype=jnp.float32))
    return weights.astype(jnp.bfloat16)


def body(groups, parts, embeddings, seed_labels, sources, counts):
    row_count = embeddings.shape[2]
    classes = seed_labels.shape[3]
    width = embeddings.shape[3]
    unit_emb = normalized(embeddings[0, 0])
    self_tile = kernel_tile(unit_emb, unit_emb, True)
    self_rows = jnp.sum(self_tile, axis=1, dtype=jnp.float32)
    centre = jnp.mean(unit_emb, axis=0, dtype=jnp.float32)
    centre_unit = centre * lax.rsqrt(jnp.sum(centre * centre) + eps)
    seed = seed_labels[0, 0]
    coarse_count = row_count // CLUS
    centre_rows = width // classes
    col_rows = row_count // classes
    steps, slots = sources.shape[2], sources.shape[3]
    me = lax.axis_index(GRP_PARTS[0])
    for axis, size in zip(GRP_PARTS[1:], parts[1:]):
        me = me * size + lax.axis_index(axis)

    def summarize(values):
        return jnp.sum(values.reshape(coarse_count, CLUS, classes), axis=1) / CLUS

    def rows_of(far):
        return jnp.broadcast_to(far[:, None, :], (coarse_count, CLUS, classes)).reshape(
            row_count, classes
        )

    after_unit = from_next(unit_emb)
    next_tile = kernel_tile(unit_emb, after_unit, False)
    next_rows = jnp.sum(next_tile, axis=1, dtype=jnp.float32)
    next_cols = jnp.sum(next_tile, axis=0, dtype=jnp.float32)

    def spread_of(labels, first):
        label_bf = labels.astype(jnp.bfloat16)
        ahead = from_next(label_bf)
        back = lax.dot_general(
            next_tile, label_bf, (((0,), (0,)), ((), ())), preferred_element_type=jnp.float32
        )
        if first:
            packet = from_prev(jnp.concatenate([back, next_cols.reshape(col_rows, classes)]))
            back_in = packet[:row_count]
            degree = self_rows + next_rows + packet[row_count:].reshape(row_count)
        else:
            back_in, degree = from_prev(back), None
        local = jnp.dot(self_tile, label_bf, preferred_element_type=jnp.float32) + jnp.dot(
            next_tile, ahead, preferred_element_type=jnp.float32
        )
        return local + back_in, degree

    local, degree = spread_of(seed, True)
    spread = local / degree[:, None]

    info = jnp.zeros((1, classes), jnp.float32)
    info = info.at[0, : steps * slots].set(sources[0, 0].reshape(-1).astype(jnp.float32))
    info = info.at[0, steps * slots].set(counts[0, 0].astype(jnp.float32))
    seed_mean = summarize(seed)
    table_a = gather_groups(
        jnp.concatenate(
            [centre_unit.reshape(centre_rows, classes), seed_mean, summarize(spread), info]
        )[None]
    )
    table = table_a[:, :centre_rows].reshape(groups, width)
    seed_means = table_a[:, centre_rows : centre_rows + coarse_count]
    spread_means = table_a[:, centre_rows + coarse_count : centre_rows + 2 * coarse_count]
    info_all = table_a[:, centre_rows + 2 * coarse_count]
    source_all = jnp.round(info_all[:, : steps * slots]).astype(jnp.int32).reshape(groups, steps, slots)
    count_all = info_all[:, steps * slots]
    pair_weight = jnp.exp(pair_scale * jnp.dot(table, table.T, precision=highest))
    member = jnp.arange(groups, dtype=jnp.int32)

    def far_all(iteration, summary):
        chosen = jnp.sum(
            (source_all[:, iteration, :, None] == member[None, None, :]).astype(jnp.float32), axis=1
        )
        coefficient = chosen * pair_weight / count_all[:, None]
        return jnp.einsum("gh,hkc->gkc", coefficient, summary, precision=highest)

    def own(values):
        return lax.dynamic_index_in_dim(values, me, axis=0, keepdims=False)

    def next_summary(spread_mean, far):
        return keep_share * seed_means + (1.0 - keep_share) * (spread_mean + far)

    far_0 = far_all(0, seed_means)
    far_1 = far_all(1, next_summary(spread_means, far_0))
    labels = keep_share * seed + (1.0 - keep_share) * (spread + rows_of(own(far_0)))

    local, _ = spread_of(labels, False)
    spread = local / degree[:, None]
    labels = keep_share * seed + (1.0 - keep_share) * (spread + rows_of(own(far_1)))
    spread_means = gather_groups(summarize(spread)[None])
    far_2 = far_all(2, next_summary(spread_means, far_1))

    local, _ = spread_of(labels, False)
    spread = local / degree[:, None]
    labels = keep_share * seed + (1.0 - keep_share) * (spread + rows_of(own(far_2)))
    return labels[None, None]


def solution(mesh):
    groups = mesh.shape["grp"]
    devices = np.asarray(mesh.devices)
    if groups % 4 == 0:
        parts = (groups // 4, 2, 2)
    else:
        parts = (groups, 1, 1)
    split = Mesh(devices.reshape((mesh.shape["seq"],) + parts), ("seq",) + GRP_PARTS)
    block = P("seq", GRP_PARTS, None, None)
    return jax.shard_map(
        lambda *args: body(groups, parts, *args),
        mesh=split,
        in_specs=(block, block, block, P("seq", GRP_PARTS)),
        out_specs=block,
        check_vma=False,
    )
```

```python
import numpy as np
import jax
import jax.numpy as jnp
from jax import lax
from jax.sharding import Mesh, PartitionSpec as P

CLUS = 32
STEPS = 3


tile_scale = 8.0
pair_scale = 2.0
keep_share = 0.2
eps = 1e-06
highest = lax.Precision.HIGHEST

GRP_PARTS = ("grp_z", "grp_y", "grp_c")


def from_next(block):
    count = lax.axis_size("seq")
    return lax.ppermute(block, "seq", [((i + 1) % count, i) for i in range(count)])


def from_prev(block):
    count = lax.axis_size("seq")
    return lax.ppermute(block, "seq", [(i, (i + 1) % count) for i in range(count)])


def gather_groups(value):
    for axis in reversed(GRP_PARTS):
        value = lax.all_gather(value, axis, axis=0, tiled=True)
    return value


def normalized(values):
    floats = values.astype(jnp.float32)
    return (floats * lax.rsqrt(jnp.sum(floats * floats, axis=-1, keepdims=True) + eps)).astype(
        jnp.bfloat16
    )


def kernel_tile(left, right, blank):
    score = jnp.dot(left, right.T, preferred_element_type=jnp.float32)
    weights = jnp.exp(tile_scale * (score - 1.0))
    if blank:
        weights = weights * (1.0 - jnp.eye(left.shape[0], dtype=jnp.float32))
    return weights.astype(jnp.bfloat16)


def body(groups, parts, embeddings, seed_labels, sources, counts):
    row_count = embeddings.shape[2]
    classes = seed_labels.shape[3]
    width = embeddings.shape[3]
    unit_emb = normalized(embeddings[0, 0])
    self_tile = kernel_tile(unit_emb, unit_emb, True)
    self_rows = jnp.sum(self_tile, axis=1, dtype=jnp.float32)
    centre = jnp.mean(unit_emb, axis=0, dtype=jnp.float32)
    centre_unit = centre * lax.rsqrt(jnp.sum(centre * centre) + eps)
    seed = seed_labels[0, 0]
    coarse_count = row_count // CLUS
    centre_rows = width // classes
    col_rows = row_count // classes
    steps, slots = sources.shape[2], sources.shape[3]
    me = lax.axis_index(GRP_PARTS[0])
    for axis, size in zip(GRP_PARTS[1:], parts[1:]):
        me = me * size + lax.axis_index(axis)

    def summarize(values):
        return jnp.sum(values.reshape(coarse_count, CLUS, classes), axis=1) / CLUS

    def rows_of(far):
        return jnp.broadcast_to(far[:, None, :], (coarse_count, CLUS, classes)).reshape(
            row_count, classes
        )

    after_unit = from_next(unit_emb)
    next_tile = kernel_tile(unit_emb, after_unit, False)
    next_rows = jnp.sum(next_tile, axis=1, dtype=jnp.float32)
    next_cols = jnp.sum(next_tile, axis=0, dtype=jnp.float32)

    def spread_of(labels, first):
        label_bf = labels.astype(jnp.bfloat16)
        ahead = from_next(label_bf)
        back = lax.dot_general(
            next_tile, label_bf, (((0,), (0,)), ((), ())), preferred_element_type=jnp.float32
        )
        if first:
            packet = from_prev(jnp.concatenate([back, next_cols.reshape(col_rows, classes)]))
            back_in = packet[:row_count]
            degree = self_rows + next_rows + packet[row_count:].reshape(row_count)
        else:
            back_in, degree = from_prev(back), None
        local = jnp.dot(self_tile, label_bf, preferred_element_type=jnp.float32) + jnp.dot(
            next_tile, ahead, preferred_element_type=jnp.float32
        )
        return local + back_in, degree

    local, degree = spread_of(seed, True)
    spread = local / degree[:, None]

    info = jnp.zeros((1, classes), jnp.float32)
    info = info.at[0, : steps * slots].set(sources[0, 0].reshape(-1).astype(jnp.float32))
    info = info.at[0, steps * slots].set(counts[0, 0].astype(jnp.float32))
    static = jnp.concatenate([centre_unit.reshape(centre_rows, classes), summarize(seed), info])
    table_0 = static[None]
    for axis in (GRP_PARTS[2], GRP_PARTS[0], GRP_PARTS[1]):
        table_0 = lax.all_gather(table_0, axis, axis=0, tiled=False)
    table_0 = jnp.swapaxes(table_0, 0, 1).reshape((groups,) + static.shape)
    table = table_0[:, :centre_rows].reshape(groups, width)
    seed_means = table_0[:, centre_rows : centre_rows + coarse_count]
    info_all = table_0[:, centre_rows + coarse_count]
    source_all = jnp.round(info_all[:, : steps * slots]).astype(jnp.int32).reshape(groups, steps, slots)
    count_all = info_all[:, steps * slots]
    pair_weight = jnp.exp(pair_scale * jnp.dot(table, table.T, precision=highest))
    member = jnp.arange(groups, dtype=jnp.int32)

    def far_all(iteration, summary):
        chosen = jnp.sum(
            (source_all[:, iteration, :, None] == member[None, None, :]).astype(jnp.float32), axis=1
        )
        coefficient = chosen * pair_weight / count_all[:, None]
        return jnp.einsum("gh,hkc->gkc", coefficient, summary, precision=highest)

    def own(values):
        return lax.dynamic_index_in_dim(values, me, axis=0, keepdims=False)

    def next_summary(spread_mean, far):
        return keep_share * seed_means + (1.0 - keep_share) * (spread_mean + far)

    far_0 = far_all(0, seed_means)
    labels = keep_share * seed + (1.0 - keep_share) * (spread + rows_of(own(far_0)))
    spread_means = gather_groups(summarize(spread)[None])
    far_1 = far_all(1, next_summary(spread_means, far_0))

    local, _ = spread_of(labels, False)
    spread = local / degree[:, None]
    labels = keep_share * seed + (1.0 - keep_share) * (spread + rows_of(own(far_1)))
    spread_means = gather_groups(summarize(spread)[None])
    far_2 = far_all(2, next_summary(spread_means, far_1))

    local, _ = spread_of(labels, False)
    spread = local / degree[:, None]
    labels = keep_share * seed + (1.0 - keep_share) * (spread + rows_of(own(far_2)))
    return labels[None, None]


def solution(mesh):
    groups = mesh.shape["grp"]
    devices = np.asarray(mesh.devices)
    if groups % 4 == 0:
        parts = (groups // 4, 2, 2)
    else:
        parts = (groups, 1, 1)
    split = Mesh(devices.reshape((mesh.shape["seq"],) + parts), ("seq",) + GRP_PARTS)
    block = P("seq", GRP_PARTS, None, None)
    return jax.shard_map(
        lambda *args: body(groups, parts, *args),
        mesh=split,
        in_specs=(block, block, block, P("seq", GRP_PARTS)),
        out_specs=block,
        check_vma=False,
    )
```

```python
import numpy as np
import jax
import jax.numpy as jnp
from jax import lax
from jax.sharding import Mesh, PartitionSpec as P

CLUS = 32
STEPS = 3


tile_scale = 8.0
pair_scale = 2.0
keep_share = 0.2
eps = 1e-06
highest = lax.Precision.HIGHEST

GRP_PARTS = ("grp_z", "grp_y", "grp_c")


def from_next(block):
    count = lax.axis_size("seq")
    return lax.ppermute(block, "seq", [((i + 1) % count, i) for i in range(count)])


def from_prev(block):
    count = lax.axis_size("seq")
    return lax.ppermute(block, "seq", [(i, (i + 1) % count) for i in range(count)])


def gather_groups(value):
    for axis in reversed(GRP_PARTS):
        value = lax.all_gather(value, axis, axis=0, tiled=True)
    return value


def normalized(values):
    floats = values.astype(jnp.float32)
    return (floats * lax.rsqrt(jnp.sum(floats * floats, axis=-1, keepdims=True) + eps)).astype(
        jnp.bfloat16
    )


def kernel_tile(left, right, blank):
    score = jnp.dot(left, right.T, preferred_element_type=jnp.float32)
    weights = jnp.exp(tile_scale * (score - 1.0))
    if blank:
        weights = weights * (1.0 - jnp.eye(left.shape[0], dtype=jnp.float32))
    return weights.astype(jnp.bfloat16)


def body(groups, parts, embeddings, seed_labels, sources, counts):
    row_count = embeddings.shape[2]
    classes = seed_labels.shape[3]
    width = embeddings.shape[3]
    unit_emb = normalized(embeddings[0, 0])
    self_tile = kernel_tile(unit_emb, unit_emb, True)
    self_rows = jnp.sum(self_tile, axis=1, dtype=jnp.float32)
    centre = jnp.mean(unit_emb, axis=0, dtype=jnp.float32)
    centre_unit = centre * lax.rsqrt(jnp.sum(centre * centre) + eps)
    seed = seed_labels[0, 0]
    coarse_count = row_count // CLUS
    centre_rows = width // classes
    col_rows = row_count // classes
    steps, slots = sources.shape[2], sources.shape[3]
    me = lax.axis_index(GRP_PARTS[0])
    for axis, size in zip(GRP_PARTS[1:], parts[1:]):
        me = me * size + lax.axis_index(axis)

    def summarize(values):
        return jnp.sum(values.reshape(coarse_count, CLUS, classes), axis=1) / CLUS

    def rows_of(far):
        return jnp.broadcast_to(far[:, None, :], (coarse_count, CLUS, classes)).reshape(
            row_count, classes
        )

    after_unit = from_next(unit_emb)
    next_tile = kernel_tile(unit_emb, after_unit, False)
    next_rows = jnp.sum(next_tile, axis=1, dtype=jnp.float32)
    next_cols = jnp.sum(next_tile, axis=0, dtype=jnp.float32)

    def spread_of(labels, first):
        label_bf = labels.astype(jnp.bfloat16)
        ahead = from_next(label_bf)
        back = lax.dot_general(
            next_tile, label_bf, (((0,), (0,)), ((), ())), preferred_element_type=jnp.float32
        )
        if first:
            packet = from_prev(jnp.concatenate([back, next_cols.reshape(col_rows, classes)]))
            back_in = packet[:row_count]
            degree = self_rows + next_rows + packet[row_count:].reshape(row_count)
        else:
            back_in, degree = from_prev(back), None
        local = jnp.dot(self_tile, label_bf, preferred_element_type=jnp.float32) + jnp.dot(
            next_tile, ahead, preferred_element_type=jnp.float32
        )
        return local + back_in, degree

    local, degree = spread_of(seed, True)
    spread = local / degree[:, None]

    info = jnp.zeros((1, classes), jnp.float32)
    info = info.at[0, : steps * slots].set(sources[0, 0].reshape(-1).astype(jnp.float32))
    info = info.at[0, steps * slots].set(counts[0, 0].astype(jnp.float32))
    seed_mean = summarize(seed)
    payload = jnp.concatenate(
        [centre_unit.reshape(centre_rows, classes), seed_mean, summarize(spread), info]
    )
    table_a = payload
    for axis in GRP_PARTS:
        table_a = lax.all_gather(table_a, axis, axis=0, tiled=False)
    table_a = jnp.transpose(table_a, (2, 1, 0, 3, 4)).reshape((groups,) + payload.shape)
    table = table_a[:, :centre_rows].reshape(groups, width)
    seed_means = table_a[:, centre_rows : centre_rows + coarse_count]
    spread_means = table_a[:, centre_rows + coarse_count : centre_rows + 2 * coarse_count]
    info_all = table_a[:, centre_rows + 2 * coarse_count]
    source_all = jnp.round(info_all[:, : steps * slots]).astype(jnp.int32).reshape(groups, steps, slots)
    count_all = info_all[:, steps * slots]
    pair_weight = jnp.exp(pair_scale * jnp.dot(table, table.T, precision=highest))
    member = jnp.arange(groups, dtype=jnp.int32)

    def far_all(iteration, summary):
        chosen = jnp.sum(
            (source_all[:, iteration, :, None] == member[None, None, :]).astype(jnp.float32), axis=1
        )
        coefficient = chosen * pair_weight / count_all[:, None]
        return jnp.einsum("gh,hkc->gkc", coefficient, summary, precision=highest)

    def own(values):
        return lax.dynamic_index_in_dim(values, me, axis=0, keepdims=False)

    def next_summary(spread_mean, far):
        return keep_share * seed_means + (1.0 - keep_share) * (spread_mean + far)

    far_0 = far_all(0, seed_means)
    far_1 = far_all(1, next_summary(spread_means, far_0))
    labels = keep_share * seed + (1.0 - keep_share) * (spread + rows_of(own(far_0)))

    local, _ = spread_of(labels, False)
    spread = local / degree[:, None]
    labels = keep_share * seed + (1.0 - keep_share) * (spread + rows_of(own(far_1)))
    spread_means = gather_groups(summarize(spread)[None])
    far_2 = far_all(2, next_summary(spread_means, far_1))

    local, _ = spread_of(labels, False)
    spread = local / degree[:, None]
    labels = keep_share * seed + (1.0 - keep_share) * (spread + rows_of(own(far_2)))
    return labels[None, None]


def solution(mesh):
    groups = mesh.shape["grp"]
    devices = np.asarray(mesh.devices)
    if groups % 4 == 0:
        parts = (groups // 4, 2, 2)
    else:
        parts = (groups, 1, 1)
    split = Mesh(devices.reshape((mesh.shape["seq"],) + parts), ("seq",) + GRP_PARTS)
    block = P("seq", GRP_PARTS, None, None)
    return jax.shard_map(
        lambda *args: body(groups, parts, *args),
        mesh=split,
        in_specs=(block, block, block, P("seq", GRP_PARTS)),
        out_specs=block,
        check_vma=False,
    )
```

```python
import numpy as np
import jax
import jax.numpy as jnp
from jax import lax
from jax.sharding import Mesh, PartitionSpec as P

CLUS = 32
STEPS = 3


tile_scale = 8.0
pair_scale = 2.0
keep_share = 0.2
eps = 1e-06
highest = lax.Precision.HIGHEST

GRP_PARTS = ("grp_z", "grp_y", "grp_c")


def from_next(block):
    count = lax.axis_size("seq")
    return lax.ppermute(block, "seq", [((i + 1) % count, i) for i in range(count)])


def from_prev(block):
    count = lax.axis_size("seq")
    return lax.ppermute(block, "seq", [(i, (i + 1) % count) for i in range(count)])


def gather_groups(value):
    value = lax.all_gather(value, GRP_PARTS[1:], axis=0, tiled=True)
    return lax.all_gather(value, GRP_PARTS[0], axis=0, tiled=True)


def normalized(values):
    floats = values.astype(jnp.float32)
    return (floats * lax.rsqrt(jnp.sum(floats * floats, axis=-1, keepdims=True) + eps)).astype(
        jnp.bfloat16
    )


def kernel_tile(left, right, blank):
    score = jnp.dot(left, right.T, preferred_element_type=jnp.float32)
    weights = jnp.exp(tile_scale * (score - 1.0))
    if blank:
        weights = weights * (1.0 - jnp.eye(left.shape[0], dtype=jnp.float32))
    return weights.astype(jnp.bfloat16)


def body(groups, parts, embeddings, seed_labels, sources, counts):
    row_count = embeddings.shape[2]
    classes = seed_labels.shape[3]
    width = embeddings.shape[3]
    unit_emb = normalized(embeddings[0, 0])
    self_tile = kernel_tile(unit_emb, unit_emb, True)
    self_rows = jnp.sum(self_tile, axis=1, dtype=jnp.float32)
    centre = jnp.mean(unit_emb, axis=0, dtype=jnp.float32)
    centre_unit = centre * lax.rsqrt(jnp.sum(centre * centre) + eps)
    seed = seed_labels[0, 0]
    coarse_count = row_count // CLUS
    centre_rows = width // classes
    col_rows = row_count // classes
    steps, slots = sources.shape[2], sources.shape[3]
    me = lax.axis_index(GRP_PARTS[0])
    for axis, size in zip(GRP_PARTS[1:], parts[1:]):
        me = me * size + lax.axis_index(axis)

    def summarize(values):
        return jnp.sum(values.reshape(coarse_count, CLUS, classes), axis=1) / CLUS

    def rows_of(far):
        return jnp.broadcast_to(far[:, None, :], (coarse_count, CLUS, classes)).reshape(
            row_count, classes
        )

    after_unit = from_next(unit_emb)
    next_tile = kernel_tile(unit_emb, after_unit, False)
    next_rows = jnp.sum(next_tile, axis=1, dtype=jnp.float32)
    next_cols = jnp.sum(next_tile, axis=0, dtype=jnp.float32)

    def spread_of(labels, first):
        label_bf = labels.astype(jnp.bfloat16)
        ahead = from_next(label_bf)
        back = lax.dot_general(
            next_tile, label_bf, (((0,), (0,)), ((), ())), preferred_element_type=jnp.float32
        )
        if first:
            packet = from_prev(jnp.concatenate([back, next_cols.reshape(col_rows, classes)]))
            back_in = packet[:row_count]
            degree = self_rows + next_rows + packet[row_count:].reshape(row_count)
        else:
            back_in, degree = from_prev(back), None
        local = jnp.dot(self_tile, label_bf, preferred_element_type=jnp.float32) + jnp.dot(
            next_tile, ahead, preferred_element_type=jnp.float32
        )
        return local + back_in, degree

    local, degree = spread_of(seed, True)
    spread = local / degree[:, None]

    info = jnp.zeros((1, classes), jnp.float32)
    info = info.at[0, : steps * slots].set(sources[0, 0].reshape(-1).astype(jnp.float32))
    info = info.at[0, steps * slots].set(counts[0, 0].astype(jnp.float32))
    seed_mean = summarize(seed)
    payload = jnp.concatenate(
        [centre_unit.reshape(centre_rows, classes), seed_mean, summarize(spread), info]
    )
    table_a = lax.all_gather(payload, GRP_PARTS[0], axis=0, tiled=False)
    table_a = lax.all_gather(table_a, GRP_PARTS[1:], axis=0, tiled=False)
    table_a = jnp.swapaxes(table_a, 0, 1).reshape((groups,) + payload.shape)
    table = table_a[:, :centre_rows].reshape(groups, width)
    seed_means = table_a[:, centre_rows : centre_rows + coarse_count]
    spread_means = table_a[:, centre_rows + coarse_count : centre_rows + 2 * coarse_count]
    info_all = table_a[:, centre_rows + 2 * coarse_count]
    source_all = jnp.round(info_all[:, : steps * slots]).astype(jnp.int32).reshape(groups, steps, slots)
    count_all = info_all[:, steps * slots]
    pair_weight = jnp.exp(pair_scale * jnp.dot(table, table.T, precision=highest))
    member = jnp.arange(groups, dtype=jnp.int32)

    def far_all(iteration, summary):
        chosen = jnp.sum(
            (source_all[:, iteration, :, None] == member[None, None, :]).astype(jnp.float32), axis=1
        )
        coefficient = chosen * pair_weight / count_all[:, None]
        return jnp.einsum("gh,hkc->gkc", coefficient, summary, precision=highest)

    def own(values):
        return lax.dynamic_index_in_dim(values, me, axis=0, keepdims=False)

    def next_summary(spread_mean, far):
        return keep_share * seed_means + (1.0 - keep_share) * (spread_mean + far)

    far_0 = far_all(0, seed_means)
    far_1 = far_all(1, next_summary(spread_means, far_0))
    labels = keep_share * seed + (1.0 - keep_share) * (spread + rows_of(own(far_0)))

    local, _ = spread_of(labels, False)
    spread = local / degree[:, None]
    labels = keep_share * seed + (1.0 - keep_share) * (spread + rows_of(own(far_1)))
    spread_means = gather_groups(summarize(spread)[None])
    far_2 = far_all(2, next_summary(spread_means, far_1))

    local, _ = spread_of(labels, False)
    spread = local / degree[:, None]
    labels = keep_share * seed + (1.0 - keep_share) * (spread + rows_of(own(far_2)))
    return labels[None, None]


def solution(mesh):
    groups = mesh.shape["grp"]
    devices = np.asarray(mesh.devices)
    if groups % 4 == 0:
        parts = (groups // 4, 2, 2)
    else:
        parts = (groups, 1, 1)
    split = Mesh(devices.reshape((mesh.shape["seq"],) + parts), ("seq",) + GRP_PARTS)
    block = P("seq", GRP_PARTS, None, None)
    return jax.shard_map(
        lambda *args: body(groups, parts, *args),
        mesh=split,
        in_specs=(block, block, block, P("seq", GRP_PARTS)),
        out_specs=block,
        check_vma=False,
    )
```

```python
import numpy as np
import jax
import jax.numpy as jnp
from jax import lax
from jax.sharding import Mesh, PartitionSpec as P

CLUS = 32
STEPS = 3


tile_scale = 8.0
pair_scale = 2.0
keep_share = 0.2
eps = 1e-06
highest = lax.Precision.HIGHEST

GRP_PARTS = ("grp_z", "grp_y", "grp_c")


def from_next(block):
    count = lax.axis_size("seq")
    return lax.ppermute(block, "seq", [((i + 1) % count, i) for i in range(count)])


def from_prev(block):
    count = lax.axis_size("seq")
    return lax.ppermute(block, "seq", [(i, (i + 1) % count) for i in range(count)])


def gather_groups(value):
    for axis in reversed(GRP_PARTS):
        value = lax.all_gather(value, axis, axis=0, tiled=True)
    return value


def normalized(values):
    floats = values.astype(jnp.float32)
    return (floats * lax.rsqrt(jnp.sum(floats * floats, axis=-1, keepdims=True) + eps)).astype(
        jnp.bfloat16
    )


def kernel_tile(left, right, blank):
    score = jnp.dot(left, right.T, preferred_element_type=jnp.float32)
    weights = jnp.exp(tile_scale * (score - 1.0))
    if blank:
        weights = weights * (1.0 - jnp.eye(left.shape[0], dtype=jnp.float32))
    return weights.astype(jnp.bfloat16)


def body(groups, parts, embeddings, seed_labels, sources, counts):
    row_count = embeddings.shape[2]
    classes = seed_labels.shape[3]
    width = embeddings.shape[3]
    unit_emb = normalized(embeddings[0, 0])
    self_tile = kernel_tile(unit_emb, unit_emb, True)
    self_rows = jnp.sum(self_tile, axis=1, dtype=jnp.float32)
    centre = jnp.mean(unit_emb, axis=0, dtype=jnp.float32)
    centre_unit = centre * lax.rsqrt(jnp.sum(centre * centre) + eps)
    seed = seed_labels[0, 0]
    coarse_count = row_count // CLUS
    centre_rows = width // classes
    col_rows = row_count // classes
    steps, slots = sources.shape[2], sources.shape[3]
    me = lax.axis_index(GRP_PARTS[0])
    for axis, size in zip(GRP_PARTS[1:], parts[1:]):
        me = me * size + lax.axis_index(axis)

    def summarize(values):
        return jnp.sum(values.reshape(coarse_count, CLUS, classes), axis=1) / CLUS

    def rows_of(far):
        return jnp.broadcast_to(far[:, None, :], (coarse_count, CLUS, classes)).reshape(
            row_count, classes
        )

    after_unit = from_next(unit_emb)
    next_tile = kernel_tile(unit_emb, after_unit, False)
    next_rows = jnp.sum(next_tile, axis=1, dtype=jnp.float32)
    next_cols = jnp.sum(next_tile, axis=0, dtype=jnp.float32)

    def spread_of(labels, first):
        label_bf = labels.astype(jnp.bfloat16)
        back = lax.dot_general(
            next_tile, label_bf, (((0,), (0,)), ((), ())), preferred_element_type=jnp.float32
        )
        if first:
            ahead = from_next(label_bf)
            packet = from_prev(jnp.concatenate([back, next_cols.reshape(col_rows, classes)]))
            back_in = packet[:row_count]
            degree = self_rows + next_rows + packet[row_count:].reshape(row_count)
        else:
            label_send, back = lax.optimization_barrier((label_bf, back))
            back_in, degree = from_prev(back), None
            ahead = from_next(label_send)
        local = jnp.dot(self_tile, label_bf, preferred_element_type=jnp.float32) + jnp.dot(
            next_tile, ahead, preferred_element_type=jnp.float32
        )
        return local + back_in, degree

    local, degree = spread_of(seed, True)
    spread = local / degree[:, None]

    info = jnp.zeros((1, classes), jnp.float32)
    info = info.at[0, : steps * slots].set(sources[0, 0].reshape(-1).astype(jnp.float32))
    info = info.at[0, steps * slots].set(counts[0, 0].astype(jnp.float32))
    seed_mean = summarize(seed)
    payload = jnp.concatenate(
        [centre_unit.reshape(centre_rows, classes), seed_mean, summarize(spread), info]
    )
    table_a = payload
    for axis in GRP_PARTS:
        table_a = lax.all_gather(table_a, axis, axis=0, tiled=False)
    table_a = jnp.transpose(table_a, (2, 1, 0, 3, 4)).reshape((groups,) + payload.shape)
    table = table_a[:, :centre_rows].reshape(groups, width)
    seed_means = table_a[:, centre_rows : centre_rows + coarse_count]
    spread_means = table_a[:, centre_rows + coarse_count : centre_rows + 2 * coarse_count]
    info_all = table_a[:, centre_rows + 2 * coarse_count]
    source_all = jnp.round(info_all[:, : steps * slots]).astype(jnp.int32).reshape(groups, steps, slots)
    count_all = info_all[:, steps * slots]
    pair_weight = jnp.exp(pair_scale * jnp.dot(table, table.T, precision=highest))
    member = jnp.arange(groups, dtype=jnp.int32)

    def far_all(iteration, summary):
        chosen = jnp.sum(
            (source_all[:, iteration, :, None] == member[None, None, :]).astype(jnp.float32), axis=1
        )
        coefficient = chosen * pair_weight / count_all[:, None]
        return jnp.einsum("gh,hkc->gkc", coefficient, summary, precision=highest)

    def own(values):
        return lax.dynamic_index_in_dim(values, me, axis=0, keepdims=False)

    def next_summary(spread_mean, far):
        return keep_share * seed_means + (1.0 - keep_share) * (spread_mean + far)

    far_0 = far_all(0, seed_means)
    far_1 = far_all(1, next_summary(spread_means, far_0))
    labels = keep_share * seed + (1.0 - keep_share) * (spread + rows_of(own(far_0)))

    local, _ = spread_of(labels, False)
    spread = local / degree[:, None]
    labels = keep_share * seed + (1.0 - keep_share) * (spread + rows_of(own(far_1)))
    spread_means = gather_groups(summarize(spread)[None])
    far_2 = far_all(2, next_summary(spread_means, far_1))

    local, _ = spread_of(labels, False)
    spread = local / degree[:, None]
    labels = keep_share * seed + (1.0 - keep_share) * (spread + rows_of(own(far_2)))
    return labels[None, None]


def solution(mesh):
    groups = mesh.shape["grp"]
    devices = np.asarray(mesh.devices)
    if groups % 4 == 0:
        parts = (groups // 4, 2, 2)
    else:
        parts = (groups, 1, 1)
    split = Mesh(devices.reshape((mesh.shape["seq"],) + parts), ("seq",) + GRP_PARTS)
    block = P("seq", GRP_PARTS, None, None)
    return jax.shard_map(
        lambda *args: body(groups, parts, *args),
        mesh=split,
        in_specs=(block, block, block, P("seq", GRP_PARTS)),
        out_specs=block,
        check_vma=False,
    )
```

```python
import numpy as np
import jax
import jax.numpy as jnp
from jax import lax
from jax.sharding import Mesh, PartitionSpec as P

CLUS = 32
STEPS = 3


tile_scale = 8.0
pair_scale = 2.0
keep_share = 0.2
eps = 1e-06
highest = lax.Precision.HIGHEST

GRP_PARTS = ("grp_z", "grp_y", "grp_c")


def from_next(block):
    count = lax.axis_size("seq")
    return lax.ppermute(block, "seq", [((i + 1) % count, i) for i in range(count)])


def from_prev(block):
    count = lax.axis_size("seq")
    return lax.ppermute(block, "seq", [(i, (i + 1) % count) for i in range(count)])


def gather_groups(value):
    for axis in reversed(GRP_PARTS):
        value = lax.all_gather(value, axis, axis=0, tiled=True)
    return value


def normalized(values):
    floats = values.astype(jnp.float32)
    return (floats * lax.rsqrt(jnp.sum(floats * floats, axis=-1, keepdims=True) + eps)).astype(
        jnp.bfloat16
    )


def kernel_tile(left, right, blank):
    score = jnp.dot(left, right.T, preferred_element_type=jnp.float32)
    weights = jnp.exp(tile_scale * (score - 1.0))
    if blank:
        weights = weights * (1.0 - jnp.eye(left.shape[0], dtype=jnp.float32))
    return weights.astype(jnp.bfloat16)


def body(groups, parts, embeddings, seed_labels, sources, counts):
    row_count = embeddings.shape[2]
    classes = seed_labels.shape[3]
    width = embeddings.shape[3]
    unit_emb = normalized(embeddings[0, 0])
    self_tile = kernel_tile(unit_emb, unit_emb, True)
    self_rows = jnp.sum(self_tile, axis=1, dtype=jnp.float32)
    centre = jnp.mean(unit_emb, axis=0, dtype=jnp.float32)
    centre_unit = centre * lax.rsqrt(jnp.sum(centre * centre) + eps)
    seed = seed_labels[0, 0]
    coarse_count = row_count // CLUS
    centre_rows = width // classes
    col_rows = row_count // classes
    steps, slots = sources.shape[2], sources.shape[3]
    me = lax.axis_index(GRP_PARTS[0])
    for axis, size in zip(GRP_PARTS[1:], parts[1:]):
        me = me * size + lax.axis_index(axis)

    def summarize(values):
        return jnp.sum(values.reshape(coarse_count, CLUS, classes), axis=1) / CLUS

    def rows_of(far):
        return jnp.broadcast_to(far[:, None, :], (coarse_count, CLUS, classes)).reshape(
            row_count, classes
        )

    after_unit = from_next(unit_emb)
    next_tile = kernel_tile(unit_emb, after_unit, False)
    next_rows = jnp.sum(next_tile, axis=1, dtype=jnp.float32)
    next_cols = jnp.sum(next_tile, axis=0, dtype=jnp.float32)

    def spread_of(labels, first, product_first=False):
        label_bf = labels.astype(jnp.bfloat16)
        back = lax.dot_general(
            next_tile, label_bf, (((0,), (0,)), ((), ())), preferred_element_type=jnp.float32
        )
        if first:
            ahead = from_next(label_bf)
            packet = from_prev(jnp.concatenate([back, next_cols.reshape(col_rows, classes)]))
            back_in = packet[:row_count]
            degree = self_rows + next_rows + packet[row_count:].reshape(row_count)
        elif product_first:
            label_send, back = lax.optimization_barrier((label_bf, back))
            back_in, degree = from_prev(back), None
            ahead = from_next(label_send)
        else:
            ahead = from_next(label_bf)
            back_in, degree = from_prev(back), None
        local = jnp.dot(self_tile, label_bf, preferred_element_type=jnp.float32) + jnp.dot(
            next_tile, ahead, preferred_element_type=jnp.float32
        )
        return local + back_in, degree

    local, degree = spread_of(seed, True)
    spread = local / degree[:, None]

    info = jnp.zeros((1, classes), jnp.float32)
    info = info.at[0, : steps * slots].set(sources[0, 0].reshape(-1).astype(jnp.float32))
    info = info.at[0, steps * slots].set(counts[0, 0].astype(jnp.float32))
    seed_mean = summarize(seed)
    payload = jnp.concatenate(
        [centre_unit.reshape(centre_rows, classes), seed_mean, summarize(spread), info]
    )
    table_a = payload
    for axis in GRP_PARTS:
        table_a = lax.all_gather(table_a, axis, axis=0, tiled=False)
    table_a = jnp.transpose(table_a, (2, 1, 0, 3, 4)).reshape((groups,) + payload.shape)
    table = table_a[:, :centre_rows].reshape(groups, width)
    seed_means = table_a[:, centre_rows : centre_rows + coarse_count]
    spread_means = table_a[:, centre_rows + coarse_count : centre_rows + 2 * coarse_count]
    info_all = table_a[:, centre_rows + 2 * coarse_count]
    source_all = jnp.round(info_all[:, : steps * slots]).astype(jnp.int32).reshape(groups, steps, slots)
    count_all = info_all[:, steps * slots]
    pair_weight = jnp.exp(pair_scale * jnp.dot(table, table.T, precision=highest))
    member = jnp.arange(groups, dtype=jnp.int32)

    def far_all(iteration, summary):
        chosen = jnp.sum(
            (source_all[:, iteration, :, None] == member[None, None, :]).astype(jnp.float32), axis=1
        )
        coefficient = chosen * pair_weight / count_all[:, None]
        return jnp.einsum("gh,hkc->gkc", coefficient, summary, precision=highest)

    def own(values):
        return lax.dynamic_index_in_dim(values, me, axis=0, keepdims=False)

    def next_summary(spread_mean, far):
        return keep_share * seed_means + (1.0 - keep_share) * (spread_mean + far)

    far_0 = far_all(0, seed_means)
    far_1 = far_all(1, next_summary(spread_means, far_0))
    labels = keep_share * seed + (1.0 - keep_share) * (spread + rows_of(own(far_0)))

    local, _ = spread_of(labels, False, True)
    spread = local / degree[:, None]
    labels = keep_share * seed + (1.0 - keep_share) * (spread + rows_of(own(far_1)))
    spread_means = gather_groups(summarize(spread)[None])
    far_2 = far_all(2, next_summary(spread_means, far_1))

    local, _ = spread_of(labels, False)
    spread = local / degree[:, None]
    labels = keep_share * seed + (1.0 - keep_share) * (spread + rows_of(own(far_2)))
    return labels[None, None]


def solution(mesh):
    groups = mesh.shape["grp"]
    devices = np.asarray(mesh.devices)
    if groups % 4 == 0:
        parts = (groups // 4, 2, 2)
    else:
        parts = (groups, 1, 1)
    split = Mesh(devices.reshape((mesh.shape["seq"],) + parts), ("seq",) + GRP_PARTS)
    block = P("seq", GRP_PARTS, None, None)
    return jax.shard_map(
        lambda *args: body(groups, parts, *args),
        mesh=split,
        in_specs=(block, block, block, P("seq", GRP_PARTS)),
        out_specs=block,
        check_vma=False,
    )
```

```python
import numpy as np
import jax
import jax.numpy as jnp
from jax import lax
from jax.sharding import Mesh, PartitionSpec as P

CLUS = 32
STEPS = 3


tile_scale = 8.0
pair_scale = 2.0
keep_share = 0.2
eps = 1e-06
highest = lax.Precision.HIGHEST

GRP_PARTS = ("grp_z", "grp_y", "grp_c")


def from_next(block):
    count = lax.axis_size("seq")
    return lax.ppermute(block, "seq", [((i + 1) % count, i) for i in range(count)])


def from_prev(block):
    count = lax.axis_size("seq")
    return lax.ppermute(block, "seq", [(i, (i + 1) % count) for i in range(count)])


def gather_z(value):
    count = lax.axis_size(GRP_PARTS[0])
    block = value.shape[0]
    held, have = value, 1
    while have < count:
        take = min(have, count - have)
        pairs = [(i, (i - have) % count) for i in range(count)]
        got = lax.ppermute(held[: take * block], GRP_PARTS[0], pairs)
        held = jnp.concatenate([held, got])
        have += take
    start = (count - lax.axis_index(GRP_PARTS[0])) % count * block
    return lax.dynamic_slice_in_dim(jnp.concatenate([held, held]), start, count * block, axis=0)


def gather_groups(value):
    for axis in reversed(GRP_PARTS[1:]):
        value = lax.all_gather(value, axis, axis=0, tiled=True)
    return gather_z(value)


def normalized(values):
    floats = values.astype(jnp.float32)
    return (floats * lax.rsqrt(jnp.sum(floats * floats, axis=-1, keepdims=True) + eps)).astype(
        jnp.bfloat16
    )


def kernel_tile(left, right, blank):
    score = jnp.dot(left, right.T, preferred_element_type=jnp.float32)
    weights = jnp.exp(tile_scale * (score - 1.0))
    if blank:
        weights = weights * (1.0 - jnp.eye(left.shape[0], dtype=jnp.float32))
    return weights.astype(jnp.bfloat16)


def body(groups, parts, embeddings, seed_labels, sources, counts):
    row_count = embeddings.shape[2]
    classes = seed_labels.shape[3]
    width = embeddings.shape[3]
    unit_emb = normalized(embeddings[0, 0])
    self_tile = kernel_tile(unit_emb, unit_emb, True)
    self_rows = jnp.sum(self_tile, axis=1, dtype=jnp.float32)
    centre = jnp.mean(unit_emb, axis=0, dtype=jnp.float32)
    centre_unit = centre * lax.rsqrt(jnp.sum(centre * centre) + eps)
    seed = seed_labels[0, 0]
    coarse_count = row_count // CLUS
    centre_rows = width // classes
    col_rows = row_count // classes
    steps, slots = sources.shape[2], sources.shape[3]
    me = lax.axis_index(GRP_PARTS[0])
    for axis, size in zip(GRP_PARTS[1:], parts[1:]):
        me = me * size + lax.axis_index(axis)

    def summarize(values):
        return jnp.sum(values.reshape(coarse_count, CLUS, classes), axis=1) / CLUS

    def rows_of(far):
        return jnp.broadcast_to(far[:, None, :], (coarse_count, CLUS, classes)).reshape(
            row_count, classes
        )

    after_unit = from_next(unit_emb)
    next_tile = kernel_tile(unit_emb, after_unit, False)
    next_rows = jnp.sum(next_tile, axis=1, dtype=jnp.float32)
    next_cols = jnp.sum(next_tile, axis=0, dtype=jnp.float32)

    def spread_of(labels, first, product_first=False):
        label_bf = labels.astype(jnp.bfloat16)
        back = lax.dot_general(
            next_tile, label_bf, (((0,), (0,)), ((), ())), preferred_element_type=jnp.float32
        )
        if first:
            ahead = from_next(label_bf)
            packet = from_prev(jnp.concatenate([back, next_cols.reshape(col_rows, classes)]))
            back_in = packet[:row_count]
            degree = self_rows + next_rows + packet[row_count:].reshape(row_count)
        elif product_first:
            label_send, back = lax.optimization_barrier((label_bf, back))
            back_in, degree = from_prev(back), None
            ahead = from_next(label_send)
        else:
            ahead = from_next(label_bf)
            back_in, degree = from_prev(back), None
        local = jnp.dot(self_tile, label_bf, preferred_element_type=jnp.float32) + jnp.dot(
            next_tile, ahead, preferred_element_type=jnp.float32
        )
        return local + back_in, degree

    local, degree = spread_of(seed, True)
    spread = local / degree[:, None]

    info = jnp.zeros((1, classes), jnp.float32)
    info = info.at[0, : steps * slots].set(sources[0, 0].reshape(-1).astype(jnp.float32))
    info = info.at[0, steps * slots].set(counts[0, 0].astype(jnp.float32))
    seed_mean = summarize(seed)
    payload = jnp.concatenate(
        [centre_unit.reshape(centre_rows, classes), seed_mean, summarize(spread), info]
    )
    table_a = gather_z(payload[None])
    for axis in GRP_PARTS[1:]:
        table_a = lax.all_gather(table_a, axis, axis=0, tiled=False)
    table_a = jnp.transpose(table_a, (2, 1, 0, 3, 4)).reshape((groups,) + payload.shape)
    table = table_a[:, :centre_rows].reshape(groups, width)
    seed_means = table_a[:, centre_rows : centre_rows + coarse_count]
    spread_means = table_a[:, centre_rows + coarse_count : centre_rows + 2 * coarse_count]
    info_all = table_a[:, centre_rows + 2 * coarse_count]
    source_all = jnp.round(info_all[:, : steps * slots]).astype(jnp.int32).reshape(groups, steps, slots)
    count_all = info_all[:, steps * slots]
    pair_weight = jnp.exp(pair_scale * jnp.dot(table, table.T, precision=highest))
    member = jnp.arange(groups, dtype=jnp.int32)

    def far_all(iteration, summary):
        chosen = jnp.sum(
            (source_all[:, iteration, :, None] == member[None, None, :]).astype(jnp.float32), axis=1
        )
        coefficient = chosen * pair_weight / count_all[:, None]
        return jnp.einsum("gh,hkc->gkc", coefficient, summary, precision=highest)

    def own(values):
        return lax.dynamic_index_in_dim(values, me, axis=0, keepdims=False)

    def next_summary(spread_mean, far):
        return keep_share * seed_means + (1.0 - keep_share) * (spread_mean + far)

    far_0 = far_all(0, seed_means)
    far_1 = far_all(1, next_summary(spread_means, far_0))
    labels = keep_share * seed + (1.0 - keep_share) * (spread + rows_of(own(far_0)))

    local, _ = spread_of(labels, False, True)
    spread = local / degree[:, None]
    labels = keep_share * seed + (1.0 - keep_share) * (spread + rows_of(own(far_1)))
    spread_means = gather_groups(summarize(spread)[None])
    far_2 = far_all(2, next_summary(spread_means, far_1))

    local, _ = spread_of(labels, False)
    spread = local / degree[:, None]
    labels = keep_share * seed + (1.0 - keep_share) * (spread + rows_of(own(far_2)))
    return labels[None, None]


def solution(mesh):
    groups = mesh.shape["grp"]
    devices = np.asarray(mesh.devices)
    if groups % 4 == 0:
        parts = (groups // 4, 2, 2)
    else:
        parts = (groups, 1, 1)
    split = Mesh(devices.reshape((mesh.shape["seq"],) + parts), ("seq",) + GRP_PARTS)
    block = P("seq", GRP_PARTS, None, None)
    return jax.shard_map(
        lambda *args: body(groups, parts, *args),
        mesh=split,
        in_specs=(block, block, block, P("seq", GRP_PARTS)),
        out_specs=block,
        check_vma=False,
    )
```

```python
import numpy as np
import jax
import jax.numpy as jnp
from jax import lax
from jax.sharding import Mesh, PartitionSpec as P

CLUS = 32
STEPS = 3


tile_scale = 8.0
pair_scale = 2.0
keep_share = 0.2
eps = 1e-06
highest = lax.Precision.HIGHEST

GRP_PARTS = ("grp_z", "grp_y", "grp_c")


def from_next(block):
    count = lax.axis_size("seq")
    return lax.ppermute(block, "seq", [((i + 1) % count, i) for i in range(count)])


def from_prev(block):
    count = lax.axis_size("seq")
    return lax.ppermute(block, "seq", [(i, (i + 1) % count) for i in range(count)])


def gather_groups(value):
    for axis in reversed(GRP_PARTS):
        value = lax.all_gather(value, axis, axis=0, tiled=True)
    return value


def normalized(values):
    floats = values.astype(jnp.float32)
    return (floats * lax.rsqrt(jnp.sum(floats * floats, axis=-1, keepdims=True) + eps)).astype(
        jnp.bfloat16
    )


def kernel_tile(left, right, blank):
    score = jnp.dot(left, right.T, preferred_element_type=jnp.float32)
    weights = jnp.exp(tile_scale * (score - 1.0))
    if blank:
        weights = weights * (1.0 - jnp.eye(left.shape[0], dtype=jnp.float32))
    return weights.astype(jnp.bfloat16)


def body(groups, parts, embeddings, seed_labels, sources, counts):
    row_count = embeddings.shape[2]
    classes = seed_labels.shape[3]
    width = embeddings.shape[3]
    unit_emb = normalized(embeddings[0, 0])
    self_tile = kernel_tile(unit_emb, unit_emb, True)
    self_rows = jnp.sum(self_tile, axis=1, dtype=jnp.float32)
    centre = jnp.mean(unit_emb, axis=0, dtype=jnp.float32)
    centre_unit = centre * lax.rsqrt(jnp.sum(centre * centre) + eps)
    seed = seed_labels[0, 0]
    coarse_count = row_count // CLUS
    centre_rows = width // classes
    col_rows = row_count // classes
    steps, slots = sources.shape[2], sources.shape[3]
    me = lax.axis_index(GRP_PARTS[0])
    for axis, size in zip(GRP_PARTS[1:], parts[1:]):
        me = me * size + lax.axis_index(axis)

    def summarize(values):
        return jnp.sum(values.reshape(coarse_count, CLUS, classes), axis=1) / CLUS

    def rows_of(far):
        return jnp.broadcast_to(far[:, None, :], (coarse_count, CLUS, classes)).reshape(
            row_count, classes
        )

    half = row_count // 2
    tiles = [kernel_tile(unit_emb, from_next(unit_emb[:half]), False)]
    tiles.append(kernel_tile(unit_emb, from_next(unit_emb[half:]), False))
    next_tile = jnp.concatenate(tiles, axis=1)
    next_rows = jnp.sum(next_tile, axis=1, dtype=jnp.float32)

    def spread_of(labels, first, product_first=False):
        label_bf = labels.astype(jnp.bfloat16)
        back = lax.dot_general(
            next_tile, label_bf, (((0,), (0,)), ((), ())), preferred_element_type=jnp.float32
        )
        if first:
            ahead = from_next(label_bf)
            back_in, prior_cols = [], []
            for tile in tiles:
                part = lax.dot_general(
                    tile, label_bf, (((0,), (0,)), ((), ())), preferred_element_type=jnp.float32
                )
                cols = jnp.sum(tile, axis=0, dtype=jnp.float32).reshape(-1, classes)
                packet = from_prev(jnp.concatenate([part, cols]))
                back_in.append(packet[: tile.shape[1]])
                prior_cols.append(packet[tile.shape[1] :].reshape(-1))
            back_in = jnp.concatenate(back_in)
            degree = self_rows + next_rows + jnp.concatenate(prior_cols)
        elif product_first:
            label_send, back = lax.optimization_barrier((label_bf, back))
            back_in, degree = from_prev(back), None
            ahead = from_next(label_send)
        else:
            ahead = from_next(label_bf)
            back_in, degree = from_prev(back), None
        local = jnp.dot(self_tile, label_bf, preferred_element_type=jnp.float32) + jnp.dot(
            next_tile, ahead, preferred_element_type=jnp.float32
        )
        return local + back_in, degree

    local, degree = spread_of(seed, True)
    spread = local / degree[:, None]

    info = jnp.zeros((1, classes), jnp.float32)
    info = info.at[0, : steps * slots].set(sources[0, 0].reshape(-1).astype(jnp.float32))
    info = info.at[0, steps * slots].set(counts[0, 0].astype(jnp.float32))
    seed_mean = summarize(seed)
    payload = jnp.concatenate(
        [centre_unit.reshape(centre_rows, classes), seed_mean, summarize(spread), info]
    )
    table_a = payload
    for axis in GRP_PARTS:
        table_a = lax.all_gather(table_a, axis, axis=0, tiled=False)
    table_a = jnp.transpose(table_a, (2, 1, 0, 3, 4)).reshape((groups,) + payload.shape)
    table = table_a[:, :centre_rows].reshape(groups, width)
    seed_means = table_a[:, centre_rows : centre_rows + coarse_count]
    spread_means = table_a[:, centre_rows + coarse_count : centre_rows + 2 * coarse_count]
    info_all = table_a[:, centre_rows + 2 * coarse_count]
    source_all = jnp.round(info_all[:, : steps * slots]).astype(jnp.int32).reshape(groups, steps, slots)
    count_all = info_all[:, steps * slots]
    pair_weight = jnp.exp(pair_scale * jnp.dot(table, table.T, precision=highest))
    member = jnp.arange(groups, dtype=jnp.int32)

    def far_all(iteration, summary):
        chosen = jnp.sum(
            (source_all[:, iteration, :, None] == member[None, None, :]).astype(jnp.float32), axis=1
        )
        coefficient = chosen * pair_weight / count_all[:, None]
        return jnp.einsum("gh,hkc->gkc", coefficient, summary, precision=highest)

    def own(values):
        return lax.dynamic_index_in_dim(values, me, axis=0, keepdims=False)

    def next_summary(spread_mean, far):
        return keep_share * seed_means + (1.0 - keep_share) * (spread_mean + far)

    far_0 = far_all(0, seed_means)
    far_1 = far_all(1, next_summary(spread_means, far_0))
    labels = keep_share * seed + (1.0 - keep_share) * (spread + rows_of(own(far_0)))

    local, _ = spread_of(labels, False, True)
    spread = local / degree[:, None]
    labels = keep_share * seed + (1.0 - keep_share) * (spread + rows_of(own(far_1)))
    spread_means = gather_groups(summarize(spread)[None])
    far_2 = far_all(2, next_summary(spread_means, far_1))

    local, _ = spread_of(labels, False)
    spread = local / degree[:, None]
    labels = keep_share * seed + (1.0 - keep_share) * (spread + rows_of(own(far_2)))
    return labels[None, None]


def solution(mesh):
    groups = mesh.shape["grp"]
    devices = np.asarray(mesh.devices)
    if groups % 4 == 0:
        parts = (groups // 4, 2, 2)
    else:
        parts = (groups, 1, 1)
    split = Mesh(devices.reshape((mesh.shape["seq"],) + parts), ("seq",) + GRP_PARTS)
    block = P("seq", GRP_PARTS, None, None)
    return jax.shard_map(
        lambda *args: body(groups, parts, *args),
        mesh=split,
        in_specs=(block, block, block, P("seq", GRP_PARTS)),
        out_specs=block,
        check_vma=False,
    )
```

```python
import numpy as np
import jax
import jax.numpy as jnp
from jax import lax
from jax.sharding import Mesh, PartitionSpec as P

CLUS = 32
STEPS = 3


tile_scale = 8.0
pair_scale = 2.0
keep_share = 0.2
eps = 1e-06
highest = lax.Precision.HIGHEST

GRP_PARTS = ("grp_z", "grp_y", "grp_c")


def from_next(block):
    count = lax.axis_size("seq")
    return lax.ppermute(block, "seq", [((i + 1) % count, i) for i in range(count)])


def from_prev(block):
    count = lax.axis_size("seq")
    return lax.ppermute(block, "seq", [(i, (i + 1) % count) for i in range(count)])


def gather_groups(value):
    for axis in reversed(GRP_PARTS):
        value = lax.all_gather(value, axis, axis=0, tiled=True)
    return value


def normalized(values):
    floats = values.astype(jnp.float32)
    return (floats * lax.rsqrt(jnp.sum(floats * floats, axis=-1, keepdims=True) + eps)).astype(
        jnp.bfloat16
    )


def kernel_tile(left, right, blank):
    score = jnp.dot(left, right.T, preferred_element_type=jnp.float32)
    weights = jnp.exp(tile_scale * (score - 1.0))
    if blank:
        weights = weights * (1.0 - jnp.eye(left.shape[0], dtype=jnp.float32))
    return weights.astype(jnp.bfloat16)


def body(groups, parts, embeddings, seed_labels, sources, counts):
    row_count = embeddings.shape[2]
    classes = seed_labels.shape[3]
    width = embeddings.shape[3]
    unit_emb = normalized(embeddings[0, 0])
    self_tile = kernel_tile(unit_emb, unit_emb, True)
    self_rows = jnp.sum(self_tile, axis=1, dtype=jnp.float32)
    centre = jnp.mean(unit_emb, axis=0, dtype=jnp.float32)
    centre_unit = centre * lax.rsqrt(jnp.sum(centre * centre) + eps)
    seed = seed_labels[0, 0]
    coarse_count = row_count // CLUS
    centre_rows = width // classes
    col_rows = row_count // classes
    steps, slots = sources.shape[2], sources.shape[3]
    me = lax.axis_index(GRP_PARTS[0])
    for axis, size in zip(GRP_PARTS[1:], parts[1:]):
        me = me * size + lax.axis_index(axis)

    def summarize(values):
        return jnp.sum(values.reshape(coarse_count, CLUS, classes), axis=1) / CLUS

    def rows_of(far):
        return jnp.broadcast_to(far[:, None, :], (coarse_count, CLUS, classes)).reshape(
            row_count, classes
        )

    seed_bf = seed.astype(jnp.bfloat16)
    arrived = from_next(jnp.concatenate([unit_emb, seed_bf], axis=1))
    after_unit, seed_ahead = arrived[:, :width], arrived[:, width:]
    next_tile = kernel_tile(unit_emb, after_unit, False)
    next_rows = jnp.sum(next_tile, axis=1, dtype=jnp.float32)
    next_cols = jnp.sum(next_tile, axis=0, dtype=jnp.float32)

    def spread_of(labels, first, product_first=False):
        label_bf = labels.astype(jnp.bfloat16)
        back = lax.dot_general(
            next_tile, label_bf, (((0,), (0,)), ((), ())), preferred_element_type=jnp.float32
        )
        if first:
            ahead = seed_ahead
            packet = from_prev(jnp.concatenate([back, next_cols.reshape(col_rows, classes)]))
            back_in = packet[:row_count]
            degree = self_rows + next_rows + packet[row_count:].reshape(row_count)
        elif product_first:
            label_send, back = lax.optimization_barrier((label_bf, back))
            back_in, degree = from_prev(back), None
            ahead = from_next(label_send)
        else:
            ahead = from_next(label_bf)
            back_in, degree = from_prev(back), None
        local = jnp.dot(self_tile, label_bf, preferred_element_type=jnp.float32) + jnp.dot(
            next_tile, ahead, preferred_element_type=jnp.float32
        )
        return local + back_in, degree

    local, degree = spread_of(seed, True)
    spread = local / degree[:, None]

    info = jnp.zeros((1, classes), jnp.float32)
    info = info.at[0, : steps * slots].set(sources[0, 0].reshape(-1).astype(jnp.float32))
    info = info.at[0, steps * slots].set(counts[0, 0].astype(jnp.float32))
    seed_mean = summarize(seed)
    payload = jnp.concatenate(
        [centre_unit.reshape(centre_rows, classes), seed_mean, summarize(spread), info]
    )
    table_a = payload
    for axis in GRP_PARTS:
        table_a = lax.all_gather(table_a, axis, axis=0, tiled=False)
    table_a = jnp.transpose(table_a, (2, 1, 0, 3, 4)).reshape((groups,) + payload.shape)
    table = table_a[:, :centre_rows].reshape(groups, width)
    seed_means = table_a[:, centre_rows : centre_rows + coarse_count]
    spread_means = table_a[:, centre_rows + coarse_count : centre_rows + 2 * coarse_count]
    info_all = table_a[:, centre_rows + 2 * coarse_count]
    source_all = jnp.round(info_all[:, : steps * slots]).astype(jnp.int32).reshape(groups, steps, slots)
    count_all = info_all[:, steps * slots]
    pair_weight = jnp.exp(pair_scale * jnp.dot(table, table.T, precision=highest))
    member = jnp.arange(groups, dtype=jnp.int32)

    def far_all(iteration, summary):
        chosen = jnp.sum(
            (source_all[:, iteration, :, None] == member[None, None, :]).astype(jnp.float32), axis=1
        )
        coefficient = chosen * pair_weight / count_all[:, None]
        return jnp.einsum("gh,hkc->gkc", coefficient, summary, precision=highest)

    def own(values):
        return lax.dynamic_index_in_dim(values, me, axis=0, keepdims=False)

    def next_summary(spread_mean, far):
        return keep_share * seed_means + (1.0 - keep_share) * (spread_mean + far)

    far_0 = far_all(0, seed_means)
    far_1 = far_all(1, next_summary(spread_means, far_0))
    labels = keep_share * seed + (1.0 - keep_share) * (spread + rows_of(own(far_0)))

    local, _ = spread_of(labels, False, True)
    spread = local / degree[:, None]
    labels = keep_share * seed + (1.0 - keep_share) * (spread + rows_of(own(far_1)))
    spread_means = gather_groups(summarize(spread)[None])
    far_2 = far_all(2, next_summary(spread_means, far_1))

    local, _ = spread_of(labels, False)
    spread = local / degree[:, None]
    labels = keep_share * seed + (1.0 - keep_share) * (spread + rows_of(own(far_2)))
    return labels[None, None]


def solution(mesh):
    groups = mesh.shape["grp"]
    devices = np.asarray(mesh.devices)
    if groups % 4 == 0:
        parts = (groups // 4, 2, 2)
    else:
        parts = (groups, 1, 1)
    split = Mesh(devices.reshape((mesh.shape["seq"],) + parts), ("seq",) + GRP_PARTS)
    block = P("seq", GRP_PARTS, None, None)
    return jax.shard_map(
        lambda *args: body(groups, parts, *args),
        mesh=split,
        in_specs=(block, block, block, P("seq", GRP_PARTS)),
        out_specs=block,
        check_vma=False,
    )
```

```python
import numpy as np
import jax
import jax.numpy as jnp
from jax import lax
from jax.sharding import Mesh, PartitionSpec as P

CLUS = 32
STEPS = 3


tile_scale = 8.0
pair_scale = 2.0
keep_share = 0.2
eps = 1e-06
highest = lax.Precision.HIGHEST

GRP_PARTS = ("grp_z", "grp_y", "grp_c")


def from_next(block):
    count = lax.axis_size("seq")
    return lax.ppermute(block, "seq", [((i + 1) % count, i) for i in range(count)])


def from_prev(block):
    count = lax.axis_size("seq")
    return lax.ppermute(block, "seq", [(i, (i + 1) % count) for i in range(count)])


def gather_groups(value):
    for axis in reversed(GRP_PARTS):
        value = lax.all_gather(value, axis, axis=0, tiled=True)
    return value


def normalized(values):
    floats = values.astype(jnp.float32)
    return (floats * lax.rsqrt(jnp.sum(floats * floats, axis=-1, keepdims=True) + eps)).astype(
        jnp.bfloat16
    )


def kernel_tile(left, right, blank):
    score = jnp.dot(left, right.T, preferred_element_type=jnp.float32)
    weights = jnp.exp(tile_scale * (score - 1.0))
    if blank:
        weights = weights * (1.0 - jnp.eye(left.shape[0], dtype=jnp.float32))
    return weights.astype(jnp.bfloat16)


def body(groups, parts, embeddings, seed_labels, sources, counts):
    row_count = embeddings.shape[2]
    classes = seed_labels.shape[3]
    width = embeddings.shape[3]
    unit_emb = normalized(embeddings[0, 0])
    self_tile = kernel_tile(unit_emb, unit_emb, True)
    self_rows = jnp.sum(self_tile, axis=1, dtype=jnp.float32)
    centre = jnp.mean(unit_emb, axis=0, dtype=jnp.float32)
    centre_unit = centre * lax.rsqrt(jnp.sum(centre * centre) + eps)
    seed = seed_labels[0, 0]
    coarse_count = row_count // CLUS
    centre_rows = width // classes
    col_rows = row_count // classes
    steps, slots = sources.shape[2], sources.shape[3]
    me = lax.axis_index(GRP_PARTS[0])
    for axis, size in zip(GRP_PARTS[1:], parts[1:]):
        me = me * size + lax.axis_index(axis)

    def summarize(values):
        return jnp.sum(values.reshape(coarse_count, CLUS, classes), axis=1) / CLUS

    def rows_of(far):
        return jnp.broadcast_to(far[:, None, :], (coarse_count, CLUS, classes)).reshape(
            row_count, classes
        )

    after_unit = from_next(unit_emb)
    next_tile = kernel_tile(unit_emb, after_unit, False)
    next_rows = jnp.sum(next_tile, axis=1, dtype=jnp.float32)
    next_cols = jnp.sum(next_tile, axis=0, dtype=jnp.float32)

    def spread_of(labels, first, product_first=False, after=None):
        label_bf = labels.astype(jnp.bfloat16)
        if after is not None:
            label_bf, after = lax.optimization_barrier((label_bf, after))
        back = lax.dot_general(
            next_tile, label_bf, (((0,), (0,)), ((), ())), preferred_element_type=jnp.float32
        )
        if first:
            ahead = from_next(label_bf)
            packet = from_prev(jnp.concatenate([back, next_cols.reshape(col_rows, classes)]))
            back_in = packet[:row_count]
            degree = self_rows + next_rows + packet[row_count:].reshape(row_count)
        elif product_first:
            label_send, back = lax.optimization_barrier((label_bf, back))
            back_in, degree = from_prev(back), None
            ahead = from_next(label_send)
        else:
            ahead = from_next(label_bf)
            back_in, degree = from_prev(back), None
        local = jnp.dot(self_tile, label_bf, preferred_element_type=jnp.float32) + jnp.dot(
            next_tile, ahead, preferred_element_type=jnp.float32
        )
        return local + back_in, degree

    local, degree = spread_of(seed, True)
    spread = local / degree[:, None]

    info = jnp.zeros((1, classes), jnp.float32)
    info = info.at[0, : steps * slots].set(sources[0, 0].reshape(-1).astype(jnp.float32))
    info = info.at[0, steps * slots].set(counts[0, 0].astype(jnp.float32))
    seed_mean = summarize(seed)
    payload = jnp.concatenate(
        [centre_unit.reshape(centre_rows, classes), seed_mean, summarize(spread), info]
    )
    table_a = payload
    for axis in GRP_PARTS:
        table_a = lax.all_gather(table_a, axis, axis=0, tiled=False)
    table_a = jnp.transpose(table_a, (2, 1, 0, 3, 4)).reshape((groups,) + payload.shape)
    table = table_a[:, :centre_rows].reshape(groups, width)
    seed_means = table_a[:, centre_rows : centre_rows + coarse_count]
    spread_means = table_a[:, centre_rows + coarse_count : centre_rows + 2 * coarse_count]
    info_all = table_a[:, centre_rows + 2 * coarse_count]
    source_all = jnp.round(info_all[:, : steps * slots]).astype(jnp.int32).reshape(groups, steps, slots)
    count_all = info_all[:, steps * slots]
    pair_weight = jnp.exp(pair_scale * jnp.dot(table, table.T, precision=highest))
    member = jnp.arange(groups, dtype=jnp.int32)

    def far_all(iteration, summary):
        chosen = jnp.sum(
            (source_all[:, iteration, :, None] == member[None, None, :]).astype(jnp.float32), axis=1
        )
        coefficient = chosen * pair_weight / count_all[:, None]
        return jnp.einsum("gh,hkc->gkc", coefficient, summary, precision=highest)

    def own(values):
        return lax.dynamic_index_in_dim(values, me, axis=0, keepdims=False)

    def next_summary(spread_mean, far):
        return keep_share * seed_means + (1.0 - keep_share) * (spread_mean + far)

    far_0 = far_all(0, seed_means)
    far_1 = far_all(1, next_summary(spread_means, far_0))
    labels = keep_share * seed + (1.0 - keep_share) * (spread + rows_of(own(far_0)))

    local, _ = spread_of(labels, False, True)
    spread = local / degree[:, None]
    labels = keep_share * seed + (1.0 - keep_share) * (spread + rows_of(own(far_1)))
    spread_means = gather_groups(summarize(spread)[None])
    far_2 = far_all(2, next_summary(spread_means, far_1))

    local, _ = spread_of(labels, False, after=spread_means)
    spread = local / degree[:, None]
    labels = keep_share * seed + (1.0 - keep_share) * (spread + rows_of(own(far_2)))
    return labels[None, None]


def solution(mesh):
    groups = mesh.shape["grp"]
    devices = np.asarray(mesh.devices)
    if groups % 4 == 0:
        parts = (groups // 4, 2, 2)
    else:
        parts = (groups, 1, 1)
    split = Mesh(devices.reshape((mesh.shape["seq"],) + parts), ("seq",) + GRP_PARTS)
    block = P("seq", GRP_PARTS, None, None)
    return jax.shard_map(
        lambda *args: body(groups, parts, *args),
        mesh=split,
        in_specs=(block, block, block, P("seq", GRP_PARTS)),
        out_specs=block,
        check_vma=False,
    )
```

```python
import numpy as np
import jax
import jax.numpy as jnp
from jax import lax
from jax.sharding import Mesh, PartitionSpec as P

CLUS = 32
STEPS = 3


tile_scale = 8.0
pair_scale = 2.0
keep_share = 0.2
eps = 1e-06
highest = lax.Precision.HIGHEST

GRP_PARTS = ("grp_z", "grp_y", "grp_c")


def from_next(block):
    count = lax.axis_size("seq")
    return lax.ppermute(block, "seq", [((i + 1) % count, i) for i in range(count)])


def from_prev(block):
    count = lax.axis_size("seq")
    return lax.ppermute(block, "seq", [(i, (i + 1) % count) for i in range(count)])


def gather_groups(value):
    for axis in reversed(GRP_PARTS):
        value = lax.all_gather(value, axis, axis=0, tiled=True)
    return value


def normalized(values):
    floats = values.astype(jnp.float32)
    return (floats * lax.rsqrt(jnp.sum(floats * floats, axis=-1, keepdims=True) + eps)).astype(
        jnp.bfloat16
    )


def kernel_tile(left, right, blank):
    score = jnp.dot(left, right.T, preferred_element_type=jnp.float32)
    weights = jnp.exp(tile_scale * (score - 1.0))
    if blank:
        weights = weights * (1.0 - jnp.eye(left.shape[0], dtype=jnp.float32))
    return weights.astype(jnp.bfloat16)


def body(groups, parts, embeddings, seed_labels, sources, counts):
    row_count = embeddings.shape[2]
    classes = seed_labels.shape[3]
    width = embeddings.shape[3]
    unit_emb = normalized(embeddings[0, 0])
    self_tile = kernel_tile(unit_emb, unit_emb, True)
    self_rows = jnp.sum(self_tile, axis=1, dtype=jnp.float32)
    centre = jnp.mean(unit_emb, axis=0, dtype=jnp.float32)
    centre_unit = centre * lax.rsqrt(jnp.sum(centre * centre) + eps)
    seed = seed_labels[0, 0]
    coarse_count = row_count // CLUS
    centre_rows = width // classes
    col_rows = row_count // classes
    steps, slots = sources.shape[2], sources.shape[3]
    me = lax.axis_index(GRP_PARTS[0])
    for axis, size in zip(GRP_PARTS[1:], parts[1:]):
        me = me * size + lax.axis_index(axis)

    def summarize(values):
        return jnp.sum(values.reshape(coarse_count, CLUS, classes), axis=1) / CLUS

    def rows_of(far):
        return jnp.broadcast_to(far[:, None, :], (coarse_count, CLUS, classes)).reshape(
            row_count, classes
        )

    after_unit = from_next(unit_emb)
    next_tile = kernel_tile(unit_emb, after_unit, False)
    next_rows = jnp.sum(next_tile, axis=1, dtype=jnp.float32)
    next_cols = jnp.sum(next_tile, axis=0, dtype=jnp.float32)

    def spread_of(labels, first, product_first=False):
        label_bf = labels.astype(jnp.bfloat16)
        back = lax.dot_general(
            next_tile, label_bf, (((0,), (0,)), ((), ())), preferred_element_type=jnp.float32
        )
        if first:
            ahead = from_next(label_bf)
            packet = from_prev(jnp.concatenate([back, next_cols.reshape(col_rows, classes)]))
            back_in = packet[:row_count]
            degree = self_rows + next_rows + packet[row_count:].reshape(row_count)
        elif product_first:
            label_send, back = lax.optimization_barrier((label_bf, back))
            back_in, degree = from_prev(back), None
            ahead = from_next(label_send)
        else:
            ahead = from_next(label_bf)
            back_in, degree = from_prev(back), None
        local = jnp.dot(self_tile, label_bf, preferred_element_type=jnp.float32) + jnp.dot(
            next_tile, ahead, preferred_element_type=jnp.float32
        )
        return local + back_in, degree

    local, degree = spread_of(seed, True)
    spread = local / degree[:, None]

    info = jnp.zeros((1, classes), jnp.float32)
    info = info.at[0, : steps * slots].set(sources[0, 0].reshape(-1).astype(jnp.float32))
    info = info.at[0, steps * slots].set(counts[0, 0].astype(jnp.float32))
    seed_mean = summarize(seed)
    payload = jnp.concatenate(
        [centre_unit.reshape(centre_rows, classes), seed_mean, summarize(spread), info]
    )
    table_a = payload
    for axis in GRP_PARTS:
        table_a = lax.all_gather(table_a, axis, axis=0, tiled=False)
    table_a = jnp.transpose(table_a, (2, 1, 0, 3, 4)).reshape((groups,) + payload.shape)
    table = table_a[:, :centre_rows].reshape(groups, width)
    seed_means = table_a[:, centre_rows : centre_rows + coarse_count]
    spread_means = table_a[:, centre_rows + coarse_count : centre_rows + 2 * coarse_count]
    info_all = table_a[:, centre_rows + 2 * coarse_count]
    source_all = jnp.round(info_all[:, : steps * slots]).astype(jnp.int32).reshape(groups, steps, slots)
    count_all = info_all[:, steps * slots]
    pair_weight = jnp.exp(pair_scale * jnp.dot(table, table.T, precision=highest))
    member = jnp.arange(groups, dtype=jnp.int32)

    def far_all(iteration, summary, own_only=False):
        chosen = jnp.sum(
            (source_all[:, iteration, :, None] == member[None, None, :]).astype(jnp.float32), axis=1
        )
        coefficient = chosen * pair_weight / count_all[:, None]
        if own_only:
            return jnp.einsum("h,hkc->kc", own(coefficient), summary, precision=highest)[None]
        return jnp.einsum("gh,hkc->gkc", coefficient, summary, precision=highest)

    def own(values):
        return lax.dynamic_index_in_dim(values, me, axis=0, keepdims=False)

    def next_summary(spread_mean, far):
        return keep_share * seed_means + (1.0 - keep_share) * (spread_mean + far)

    far_0 = far_all(0, seed_means)
    far_1 = far_all(1, next_summary(spread_means, far_0))
    labels = keep_share * seed + (1.0 - keep_share) * (spread + rows_of(own(far_0)))

    local, _ = spread_of(labels, False, True)
    spread = local / degree[:, None]
    labels = keep_share * seed + (1.0 - keep_share) * (spread + rows_of(own(far_1)))
    spread_means = gather_groups(summarize(spread)[None])
    far_2 = far_all(2, next_summary(spread_means, far_1), own_only=True)

    local, _ = spread_of(labels, False)
    spread = local / degree[:, None]
    labels = keep_share * seed + (1.0 - keep_share) * (spread + rows_of(far_2[0]))
    return labels[None, None]


def solution(mesh):
    groups = mesh.shape["grp"]
    devices = np.asarray(mesh.devices)
    if groups % 4 == 0:
        parts = (groups // 4, 2, 2)
    else:
        parts = (groups, 1, 1)
    split = Mesh(devices.reshape((mesh.shape["seq"],) + parts), ("seq",) + GRP_PARTS)
    block = P("seq", GRP_PARTS, None, None)
    return jax.shard_map(
        lambda *args: body(groups, parts, *args),
        mesh=split,
        in_specs=(block, block, block, P("seq", GRP_PARTS)),
        out_specs=block,
        check_vma=False,
    )
```

```python
import numpy as np
import jax
import jax.numpy as jnp
from jax import lax
from jax.sharding import Mesh, PartitionSpec as P

CLUS = 32
STEPS = 3


tile_scale = 8.0
pair_scale = 2.0
keep_share = 0.2
eps = 1e-06
highest = lax.Precision.HIGHEST

GRP_PARTS = ("grp_z", "grp_y", "grp_c")


def from_next(block):
    count = lax.axis_size("seq")
    return lax.ppermute(block, "seq", [((i + 1) % count, i) for i in range(count)])


def from_prev(block):
    count = lax.axis_size("seq")
    return lax.ppermute(block, "seq", [(i, (i + 1) % count) for i in range(count)])


def gather_groups(value):
    for axis in reversed(GRP_PARTS):
        value = lax.all_gather(value, axis, axis=0, tiled=True)
    return value


def normalized(values):
    floats = values.astype(jnp.float32)
    return (floats * lax.rsqrt(jnp.sum(floats * floats, axis=-1, keepdims=True) + eps)).astype(
        jnp.bfloat16
    )


def kernel_tile(left, right, blank):
    score = jnp.dot(left, right.T, preferred_element_type=jnp.float32)
    weights = jnp.exp(tile_scale * (score - 1.0))
    if blank:
        weights = weights * (1.0 - jnp.eye(left.shape[0], dtype=jnp.float32))
    return weights.astype(jnp.bfloat16)


def body(groups, parts, embeddings, seed_labels, sources, counts):
    row_count = embeddings.shape[2]
    classes = seed_labels.shape[3]
    width = embeddings.shape[3]
    unit_emb = normalized(embeddings[0, 0])
    self_tile = kernel_tile(unit_emb, unit_emb, True)
    self_rows = jnp.sum(self_tile, axis=1, dtype=jnp.float32)
    centre = jnp.mean(unit_emb, axis=0, dtype=jnp.float32)
    centre_unit = centre * lax.rsqrt(jnp.sum(centre * centre) + eps)
    seed = seed_labels[0, 0]
    coarse_count = row_count // CLUS
    centre_rows = width // classes
    col_rows = row_count // classes
    steps, slots = sources.shape[2], sources.shape[3]
    me = lax.axis_index(GRP_PARTS[0])
    for axis, size in zip(GRP_PARTS[1:], parts[1:]):
        me = me * size + lax.axis_index(axis)

    def summarize(values):
        return jnp.sum(values.reshape(coarse_count, CLUS, classes), axis=1) / CLUS

    def rows_of(far):
        return jnp.broadcast_to(far[:, None, :], (coarse_count, CLUS, classes)).reshape(
            row_count, classes
        )

    after_unit = from_next(unit_emb)
    next_tile = kernel_tile(unit_emb, after_unit, False)
    next_rows = jnp.sum(next_tile, axis=1, dtype=jnp.float32)
    next_cols = jnp.sum(next_tile, axis=0, dtype=jnp.float32)

    def spread_of(labels, first, product_first=False):
        label_bf = labels.astype(jnp.bfloat16)
        back = lax.dot_general(
            next_tile, label_bf, (((0,), (0,)), ((), ())), preferred_element_type=jnp.float32
        )
        if first:
            ahead = from_next(label_bf)
            packet = from_prev(jnp.concatenate([back, next_cols.reshape(col_rows, classes)]))
            back_in = packet[:row_count]
            degree = self_rows + next_rows + packet[row_count:].reshape(row_count)
        elif product_first:
            label_send, back = lax.optimization_barrier((label_bf, back))
            back_in, degree = from_prev(back), None
            ahead = from_next(label_send)
        else:
            ahead = from_next(label_bf)
            back_in, degree = from_prev(back), None
        local = jnp.dot(self_tile, label_bf, preferred_element_type=jnp.float32) + jnp.dot(
            next_tile, ahead, preferred_element_type=jnp.float32
        )
        return local + back_in, degree

    local, degree = spread_of(seed, True)
    spread = local / degree[:, None]

    info = jnp.zeros((1, classes), jnp.float32)
    info = info.at[0, : steps * slots].set(sources[0, 0].reshape(-1).astype(jnp.float32))
    info = info.at[0, steps * slots].set(counts[0, 0].astype(jnp.float32))
    seed_mean = summarize(seed)
    payload = jnp.concatenate(
        [centre_unit.reshape(centre_rows, classes), seed_mean, summarize(spread), info]
    )
    table_a = payload
    for axis in (GRP_PARTS[2], GRP_PARTS[0], GRP_PARTS[1]):
        table_a = lax.all_gather(table_a, axis, axis=0, tiled=False)
    table_a = jnp.transpose(table_a, (1, 0, 2, 3, 4)).reshape((groups,) + payload.shape)
    table = table_a[:, :centre_rows].reshape(groups, width)
    seed_means = table_a[:, centre_rows : centre_rows + coarse_count]
    spread_means = table_a[:, centre_rows + coarse_count : centre_rows + 2 * coarse_count]
    info_all = table_a[:, centre_rows + 2 * coarse_count]
    source_all = jnp.round(info_all[:, : steps * slots]).astype(jnp.int32).reshape(groups, steps, slots)
    count_all = info_all[:, steps * slots]
    pair_weight = jnp.exp(pair_scale * jnp.dot(table, table.T, precision=highest))
    member = jnp.arange(groups, dtype=jnp.int32)

    def far_all(iteration, summary):
        chosen = jnp.sum(
            (source_all[:, iteration, :, None] == member[None, None, :]).astype(jnp.float32), axis=1
        )
        coefficient = chosen * pair_weight / count_all[:, None]
        return jnp.einsum("gh,hkc->gkc", coefficient, summary, precision=highest)

    def own(values):
        return lax.dynamic_index_in_dim(values, me, axis=0, keepdims=False)

    def next_summary(spread_mean, far):
        return keep_share * seed_means + (1.0 - keep_share) * (spread_mean + far)

    far_0 = far_all(0, seed_means)
    far_1 = far_all(1, next_summary(spread_means, far_0))
    labels = keep_share * seed + (1.0 - keep_share) * (spread + rows_of(own(far_0)))

    local, _ = spread_of(labels, False, True)
    spread = local / degree[:, None]
    labels = keep_share * seed + (1.0 - keep_share) * (spread + rows_of(own(far_1)))
    spread_means = gather_groups(summarize(spread)[None])
    far_2 = far_all(2, next_summary(spread_means, far_1))

    local, _ = spread_of(labels, False)
    spread = local / degree[:, None]
    labels = keep_share * seed + (1.0 - keep_share) * (spread + rows_of(own(far_2)))
    return labels[None, None]


def solution(mesh):
    groups = mesh.shape["grp"]
    devices = np.asarray(mesh.devices)
    if groups % 4 == 0:
        parts = (groups // 4, 2, 2)
    else:
        parts = (groups, 1, 1)
    split = Mesh(devices.reshape((mesh.shape["seq"],) + parts), ("seq",) + GRP_PARTS)
    block = P("seq", GRP_PARTS, None, None)
    return jax.shard_map(
        lambda *args: body(groups, parts, *args),
        mesh=split,
        in_specs=(block, block, block, P("seq", GRP_PARTS)),
        out_specs=block,
        check_vma=False,
    )
```
